256 devices in a mesh: slab: 4 (over x), dev: 64 (over y, z, core).
Axes of the slice: x: 4, y: 4, z: 8, core: 2. Of those that a mesh axis runs over, the one named last changes fastest.
Arguments:
- pixels: bfloat16 [12288, 384], P(('slab', 'dev')), may hold values from -14 to 14
- tile_clip: int32 [12288], P(('slab', 'dev')), may hold values from 0 to 511, never falling along the last dimension, each value on 1 to 72 neighbouring positions
- tile_encoder: int32 [12288, 1], P(('slab', 'dev')), may hold values from 0 to 63; in each aligned block of 48 rows (0 to 47, 48 to 95, ...) at most 2 rows name the same one
- slot_owner: int32 [32768, 1], P(('slab', 'dev')), may hold values from 0 to 63; in each aligned block of 128 rows (0 to 127, 128 to 255, ...) at most 2 rows name the same one
- conv_first: bfloat16 [3, 3, 3, 3, 128], replicated, may hold values from -0.625 to 0.625
- gain_first: float32 [128], replicated, may hold values from 0.25 to 1.75
- bias_first: float32 [128], replicated, may hold values from -2.5 to 2.5
- conv_down: bfloat16 [3, 3, 3, 128, 256], replicated, may hold values from -0.109375 to 0.109375
- gain_second: float32 [256], replicated, may hold values from 0.25 to 1.75
- bias_second: float32 [256], replicated, may hold values from -2.5 to 2.5
- project: bfloat16 [256, 128], replicated, may hold values from -0.375 to 0.375
- project_bias: float32 [128], replicated, may hold values from -2.5 to 2.5
Outputs:
- packed: bfloat16 [1048576, 128], P(('slab', 'dev'))
The draws below stay inside these ranges and needn't reach their ends.
Inputs may be any that keep to these rules, and one draw needn't show every extreme that they name: `tile_encoder`: no loader sends more than 2 of its tiles to one encoder. `slot_owner`: the 128 slots of each encoder name every owner exactly 2 times. `tile_clip`: every clip has at least one tile.
All inputs are finite; a program needn't handle non-finite values.
Results may differ from the reference program's by a relative error of at most 0.0061.
Values may be sent and summed in bfloat16 or wider, within the bound.
No kernel may reach another device: no remote copies, remote signals or barrier semaphores. Data moves between devices by JAX's collectives and lax.ppermute only.
A program may use at most 64 MiB of HBM per device.

```python
import math
import jax
import jax.numpy as jnp
import numpy as np
from jax import lax

C1 = 128
C2 = 256
LAT = 128
GROUPS = 32
FR = 2
HT = 8
WT = 8
TILE_LD = 48
CAP = 2
ENC_SLOTS = 128
TILES = 12288
ALL_SLOTS = 32768
CLIPS = 512
CLIP_MOST = 72
PIX = 384
LROWS = 32
N_SLAB = 4
N_DEV = 64


def draw_pixels(key, part):
    first_key, second_key, third_key = jax.random.split(key, 3)
    base = jnp.clip(jax.random.normal(first_key, (TILES, PIX), jnp.float32), -4.0, 4.0)
    scales = jnp.exp(jax.random.uniform(second_key, (TILES, 1), jnp.float32, math.log(0.3), math.log(3.0)))
    offsets = jax.random.uniform(third_key, (TILES, 1), jnp.float32, -1.0, 1.0)
    return (base * scales + offsets).astype(jnp.bfloat16)


def profile(number_of, total, most, lean):
    loads = [(1 << 20) // math.isqrt(rank ** lean) + 1 for rank in range(2, number_of + 1)]
    surplus, holding = total - most - (number_of - 1), [1] * (number_of - 1)
    while surplus > 0:
        free = [i for i in range(number_of - 1) if holding[i] < most]
        mass, budget = sum([loads[i] for i in free]), surplus
        for i in free:
            extra = min(most - holding[i], max(1, budget * loads[i] // mass), surplus)
            holding[i] = holding[i] + extra
            surplus = surplus - extra
    return np.array([most] + holding)


def uneven_parts(key, count, total, limit, skew):
    if count == 2:
        one = jax.random.randint(key, (), max(1, total - limit), min(limit, total - 1) + 1)
        return jnp.stack([one, total - one])
    tallies = jnp.asarray(profile(count, total, limit, skew), jnp.int32)
    twos = (count - 1) // 2
    giver, sink = tallies[1:1 + 2 * twos:2], tallies[2:2 + 2 * twos:2]
    room = jnp.minimum(giver - 1, limit - sink)
    shifted = jax.random.randint(jax.random.fold_in(key, 1), (twos,), 0, 1 << 20) % (room + 1)
    tallies = tallies.at[1:1 + 2 * twos:2].set(giver - shifted).at[2:2 + 2 * twos:2].set(sink + shifted)
    return tallies[jax.random.permutation(jax.random.fold_in(key, 2), count)]


def shared_out(own_key, own, number, rows, count, top, limit, slope):
    sequence = jax.random.permutation(own_key, count)
    heavy_load, common = portions_of(count, rows * top, limit, slope, True), portions_of(count, rows * top, limit, slope, False)
    places = jnp.arange(count)

    def named(lengths, rotation):
        used = int((lengths > 0).sum())
        fixed = max(1, used // 4)
        passed = fixed + (places - fixed + rotation * (used - fixed)) % max(1, count - fixed)
        return jnp.zeros((count,), jnp.int32).at[sequence[jnp.where(places < fixed, places, passed)]].set(jnp.asarray(lengths, jnp.int32))

    lengths = jnp.where(number % 4 == 0, named(heavy_load, number // 4), named(common, number - number // 4 - 1))
    mixed = jax.random.permutation(jax.random.fold_in(own, 3), count)
    donor, sink = mixed[0:count // 2 * 2:2], mixed[1:count // 2 * 2:2]
    margin = jnp.minimum(lengths[donor] - 1, limit - lengths[sink]) // 2
    margin = jnp.where((donor == sequence[0]) | (sink == sequence[0]) | (lengths[sink] == 0), 0, jnp.maximum(margin, 0))
    passed = jax.random.randint(jax.random.fold_in(own, 4), (count // 2,), 0, 1 << 20) % (margin + 1)
    lengths = lengths.at[donor].add(-passed).at[sink].add(passed)
    items = jnp.searchsorted(jnp.cumsum(lengths), jnp.arange(rows * top), side="right").astype(jnp.int32)
    grid = items.reshape(top, rows).T
    grid = grid[jax.random.permutation(jax.random.fold_in(own, 1), rows)]
    rotation = jax.random.randint(jax.random.fold_in(own, 2), (rows, 1), 0, top)
    return jnp.take_along_axis(grid, (jnp.arange(top)[None, :] + rotation) % top, axis=1)


def portions_of(count, total, limit, skew, full):
    loads = [(1 << 20) // math.isqrt(standing ** skew) + 1 for standing in range(1, count + 1)]
    largest = limit if full else min(limit, max(-(-total // count), total * loads[0] // sum(loads)))
    least = 1 if total - largest >= count - 1 else 0
    counts, surplus = [largest] + [least] * (count - 1), total - largest - least * (count - 1)
    while surplus > 0:
        free = [i for i in range(1, count) if counts[i] < largest] or [i for i in range(1, count) if counts[i] < limit]
        whole, left = sum([loads[i] for i in free]), surplus
        for i in free:
            more = min(limit - counts[i], max(1, left * loads[i] // whole), surplus)
            counts[i] = counts[i] + more
            surplus = surplus - more
    return np.array(counts)


def bell_draw(key, dims, spread, limit, kind=jnp.bfloat16):
    return jnp.clip(spread * jax.random.normal(key, dims, jnp.float32), -limit, limit).astype(kind)


def setup_inputs(seed: int = 0) -> dict:
    splits = jax.random.split(jax.random.key(seed), 13)
    pixels = draw_pixels(jax.random.fold_in(splits[12], 71), 0)
    tile_clip = jnp.searchsorted(jnp.cumsum(uneven_parts(splits[1], CLIPS, TILES, CLIP_MOST, 2)), jnp.arange(TILES), side="right").astype(jnp.int32)
    tile_encoder_keys = jax.random.split(jax.random.fold_in(splits[2], 1), TILES // TILE_LD)
    tile_encoder_turns = jax.random.permutation(jax.random.fold_in(splits[2], 3), TILES // TILE_LD)
    tile_encoder = jax.vmap(lambda own, number: shared_out(jax.random.fold_in(splits[2], 2), own, number, TILE_LD, N_DEV, 1, CAP, 2))(tile_encoder_keys, tile_encoder_turns).reshape((TILES, 1))
    slot_owner_keys = jax.random.split(jax.random.fold_in(splits[3], 1), ALL_SLOTS // ENC_SLOTS)
    slot_owner_turns = jax.random.permutation(jax.random.fold_in(splits[3], 3), ALL_SLOTS // ENC_SLOTS)
    slot_owner = jax.vmap(lambda own, number: shared_out(jax.random.fold_in(splits[3], 2), own, number, ENC_SLOTS, N_DEV, 1, CAP, 0))(slot_owner_keys, slot_owner_turns).reshape((ALL_SLOTS, 1))
    conv_first = bell_draw(splits[4], (3, 3, 3, 3, C1), 81 ** -0.5, 0.625)
    gain_first = jnp.clip(1.0 + 0.15 * jax.random.normal(splits[5], (C1,), jnp.float32), 0.25, 1.75)
    bias_first = bell_draw(splits[6], (C1,), 0.5, 2.5, jnp.float32)
    conv_down = bell_draw(splits[7], (3, 3, 3, C1, C2), (27 * C1) ** -0.5, 0.109375)
    gain_second = jnp.clip(1.0 + 0.15 * jax.random.normal(splits[8], (C2,), jnp.float32), 0.25, 1.75)
    bias_second = bell_draw(splits[9], (C2,), 0.5, 2.5, jnp.float32)
    project = bell_draw(splits[10], (C2, LAT), C2 ** -0.5, 0.375)
    project_bias = bell_draw(splits[11], (LAT,), 0.5, 2.5, jnp.float32)
    return {"pixels": pixels, "tile_clip": tile_clip, "tile_encoder": tile_encoder, "slot_owner": slot_owner, "conv_first": conv_first, "gain_first": gain_first, "bias_first": bias_first, "conv_down": conv_down, "gain_second": gain_second, "bias_second": bias_second, "project": project, "project_bias": project_bias}


epsilon = 1e-05
layout = ('NDHWC', 'DHWIO', 'NDHWC')

def conv_exact(inputs, kernel, stride):
    return lax.conv_general_dilated(inputs.astype(jnp.float32), kernel.astype(jnp.float32), (1, stride, stride), ((2, 0), (1, 1), (1, 1)), dimension_numbers=layout, precision=lax.Precision.HIGHEST)

def group_sums(values):
    tiles = values.shape[0]
    width = values.shape[-1]
    grouped = values.reshape(tiles, -1, GROUPS, width // GROUPS)
    return (lax.optimization_barrier(jnp.sum(grouped, axis=(1, 3))), lax.optimization_barrier(jnp.sum(grouped * grouped, axis=(1, 3))))

def clip_params(sums, squares, tile_clip, per_tile):
    totals = jax.ops.segment_sum(sums, tile_clip, CLIPS)
    totals_sq = jax.ops.segment_sum(squares, tile_clip, CLIPS)
    tile_count = jax.ops.segment_sum(jnp.ones(tile_clip.shape, jnp.float32), tile_clip, CLIPS)
    voxels = tile_count * per_tile
    means = totals / voxels[:, None]
    variance = totals_sq / voxels[:, None] - means * means
    return (means[tile_clip], lax.rsqrt(variance + epsilon)[tile_clip])

def normalize(values, means, scales, gain, offset):
    tiles = values.shape[0]
    width = values.shape[-1]
    grouped = values.astype(jnp.float32).reshape(tiles, -1, GROUPS, width // GROUPS)
    scaled = (grouped - means[:, None, :, None]) * scales[:, None, :, None]
    result = scaled.reshape(values.shape) * gain + offset
    return jax.nn.silu(result).astype(jnp.bfloat16)

def arrival_rank(targets):
    order = jnp.arange(targets.shape[-1])
    earlier = (targets[..., None, :] == targets[..., :, None]) & (order[None, :] < order[:, None])
    return lax.optimization_barrier(jnp.sum(earlier.astype(jnp.int32), axis=-1)).astype(jnp.int32)

def reference(pixels, tile_clip, tile_encoder, slot_owner, conv_first, gain_first, bias_first, conv_down, gain_second, bias_second, project, project_bias):
    block_size = math.gcd(64, TILES)
    blocks = TILES // block_size
    tiles = pixels.reshape(blocks, block_size, FR, HT, WT, 3)

    def first_section(inputs):
        hidden = conv_exact(inputs, conv_first, 1).astype(jnp.bfloat16)
        sums, squares = group_sums(hidden.astype(jnp.float32))
        return (hidden, sums, squares)
    first_out, sums_a, squares_a = lax.map(first_section, tiles)
    means_a, scales_a = clip_params(sums_a.reshape(TILES, GROUPS), squares_a.reshape(TILES, GROUPS), tile_clip, FR * HT * WT * (C1 // GROUPS))

    def second_section(packet):
        hidden, means, scales = packet
        active = normalize(hidden, means, scales, gain_first, bias_first)
        down = conv_exact(active, conv_down, 2).astype(jnp.bfloat16)
        sums, squares = group_sums(down.astype(jnp.float32))
        return (down, sums, squares)
    second_out, sums_b, squares_b = lax.map(second_section, (first_out, means_a.reshape(blocks, block_size, GROUPS), scales_a.reshape(blocks, block_size, GROUPS)))
    means_b, scales_b = clip_params(sums_b.reshape(TILES, GROUPS), squares_b.reshape(TILES, GROUPS), tile_clip, LROWS * (C2 // GROUPS))

    def third_section(packet):
        hidden, means, scales = packet
        active = normalize(hidden, means, scales, gain_second, bias_second)
        flat = active.reshape(-1, C2)
        latent = jnp.dot(flat, project, preferred_element_type=jnp.float32) + project_bias
        return latent.astype(jnp.bfloat16).reshape(block_size, LROWS, LAT)
    latents = lax.map(third_section, (second_out, means_b.reshape(blocks, block_size, GROUPS), scales_b.reshape(blocks, block_size, GROUPS))).reshape(TILES, LROWS, LAT)
    loaders = N_SLAB * N_DEV
    encoder = tile_encoder[:, 0].reshape(loaders, TILE_LD)
    rank = arrival_rank(encoder)
    device_id = jnp.arange(loaders, dtype=jnp.int32)[:, None]
    slot = (device_id // N_DEV * N_DEV + encoder) * ENC_SLOTS + device_id % N_DEV * CAP + rank
    owner = slot_owner[:, 0].reshape(loaders, ENC_SLOTS)
    owner_rank = arrival_rank(owner)
    target = (device_id // N_DEV * N_DEV + owner) * ENC_SLOTS + device_id % N_DEV * CAP + owner_rank
    destination = target.reshape(-1)[slot.reshape(-1)].astype(jnp.int32)
    packed = jnp.zeros((ALL_SLOTS, LROWS, LAT), jnp.bfloat16).at[destination].set(latents)
    return packed.reshape(ALL_SLOTS * LROWS, LAT)
```

```python
import jax
import jax.numpy as jnp
from jax import lax
from jax.sharding import PartitionSpec as P

C1 = 128
C2 = 256
LAT = 128
GROUPS = 32
FR = 2
HT = 8
WT = 8
LROWS = 32
AXES = ("slab", "dev")


epsilon = 1e-05
layout = ("NDHWC", "DHWIO", "NDHWC")
precise = lax.Precision.HIGHEST


def conv_local(inputs, kernel, stride):
    return lax.conv_general_dilated(
        inputs,
        kernel,
        (1, stride, stride),
        ((2, 0), (1, 1), (1, 1)),
        dimension_numbers=layout,
        preferred_element_type=jnp.float32,
    )


def group_sums(values):
    tiles = values.shape[0]
    width = values.shape[-1]
    grouped = values.reshape(tiles, -1, GROUPS, width // GROUPS)
    return (jnp.sum(grouped, axis=(1, 3)), jnp.sum(grouped * grouped, axis=(1, 3)))


def shifted(x, shift, n):
    if shift > 0:
        perm = [(i, i + shift) for i in range(n - shift)]
    else:
        perm = [(i, i + shift) for i in range(-shift, n)]
    return lax.ppermute(x, AXES, perm)


def clip_totals(clips, stats):
    n = lax.axis_size("slab") * lax.axis_size("dev")
    member = (clips[:, None] == clips[None, :]).astype(jnp.float32)
    own = jnp.dot(member, stats, precision=precise)
    clip_f = clips.astype(jnp.float32)
    to_right = jnp.concatenate([clip_f[-1:], own[-1]])[None, :]
    to_left = jnp.concatenate([clip_f[:1], own[0]])[None, :]
    received = jnp.concatenate(
        [
            shifted(to_right, 1, n),
            shifted(to_right, 2, n),
            shifted(to_left, -1, n),
            shifted(to_left, -2, n),
        ],
        axis=0,
    )
    match = (clip_f[:, None] == received[None, :, 0]).astype(jnp.float32)
    return own + jnp.dot(match, received[:, 1:], precision=precise)


def finish_stats(totals, per_tile):
    voxels = totals[:, -1:] * per_tile
    means = totals[:, :GROUPS] / voxels
    variance = totals[:, GROUPS : 2 * GROUPS] / voxels - means * means
    return (means, lax.rsqrt(variance + epsilon))


def normalize(values, means, scales, gain, offset):
    tiles = values.shape[0]
    width = values.shape[-1]
    grouped = values.astype(jnp.float32).reshape(tiles, -1, GROUPS, width // GROUPS)
    scaled = (grouped - means[:, None, :, None]) * scales[:, None, :, None]
    result = scaled.reshape(values.shape) * gain + offset
    return jax.nn.silu(result).astype(jnp.bfloat16)


def arrival_rank(targets):
    order = jnp.arange(targets.shape[0])
    earlier = (targets[None, :] == targets[:, None]) & (order[None, :] < order[:, None])
    return jnp.sum(earlier.astype(jnp.int32), axis=1)


def encode(tiles, clips, weights):
    (
        conv_first,
        gain_first,
        bias_first,
        conv_down,
        gain_second,
        bias_second,
        project,
        project_bias,
    ) = weights
    how_many = tiles.shape[0]
    ones = jnp.ones((how_many, 1), jnp.float32)

    hidden = conv_local(tiles, conv_first, 1).astype(jnp.bfloat16)
    sums, squares = group_sums(hidden.astype(jnp.float32))
    totals = clip_totals(clips, jnp.concatenate([sums, squares, ones], axis=1))
    means, scales = finish_stats(totals, FR * HT * WT * (C1 // GROUPS))
    active = normalize(hidden, means, scales, gain_first, bias_first)

    down = conv_local(active, conv_down, 2).astype(jnp.bfloat16)
    sums, squares = group_sums(down.astype(jnp.float32))
    totals = clip_totals(clips, jnp.concatenate([sums, squares, ones], axis=1))
    means, scales = finish_stats(totals, LROWS * (C2 // GROUPS))
    active = normalize(down, means, scales, gain_second, bias_second)

    flat = active.reshape(-1, C2)
    latent = jnp.dot(flat, project, preferred_element_type=jnp.float32) + project_bias
    return latent.astype(jnp.bfloat16).reshape(how_many, LROWS, LAT)


def per_device(
    pixels,
    tile_clip,
    tile_encoder,
    slot_owner,
    conv_first,
    gain_first,
    bias_first,
    conv_down,
    gain_second,
    bias_second,
    project,
    project_bias,
):
    weights = (
        conv_first,
        gain_first,
        bias_first,
        conv_down,
        gain_second,
        bias_second,
        project,
        project_bias,
    )
    group_width = lax.axis_size("dev")
    slots = slot_owner.shape[0]
    capacity = slots // group_width
    encoder = tile_encoder[:, 0]
    owner = slot_owner[:, 0]
    place = encoder * capacity + arrival_rank(encoder)
    target = owner * capacity + arrival_rank(owner)

    tiles = pixels.reshape(pixels.shape[0], FR, HT, WT, 3)
    latents = encode(tiles, tile_clip, weights)

    outgoing = jnp.zeros((slots, LROWS, LAT), jnp.bfloat16).at[place].set(latents)
    arrived = lax.all_to_all(
        outgoing.reshape(group_width, capacity, LROWS, LAT),
        "dev",
        split_axis=0,
        concat_axis=0,
        tiled=True,
    ).reshape(slots, LROWS, LAT)
    forward = jnp.zeros((slots, LROWS, LAT), jnp.bfloat16).at[target].set(arrived)
    received = lax.all_to_all(
        forward.reshape(group_width, capacity, LROWS, LAT),
        "dev",
        split_axis=0,
        concat_axis=0,
        tiled=True,
    )
    return received.reshape(slots * LROWS, LAT)


def solution(mesh):
    in_specs = (
        P(AXES, None),
        P(AXES),
        P(AXES, None),
        P(AXES, None),
        P(),
        P(),
        P(),
        P(),
        P(),
        P(),
        P(),
        P(),
    )
    out_specs = P(AXES, None)
    return jax.shard_map(
        per_device, mesh=mesh, in_specs=in_specs, out_specs=out_specs, check_vma=False
    )
```

```python
import jax
import jax.numpy as jnp
from jax import lax
from jax.sharding import PartitionSpec as P

C1 = 128
C2 = 256
LAT = 128
GROUPS = 32
FR = 2
HT = 8
WT = 8
LROWS = 32
AXES = ("slab", "dev")


epsilon = 1e-05
layout = ("NDHWC", "DHWIO", "NDHWC")
precise = lax.Precision.HIGHEST


def conv_local(inputs, kernel, stride):
    return lax.conv_general_dilated(
        inputs,
        kernel,
        (1, stride, stride),
        ((2, 0), (1, 1), (1, 1)),
        dimension_numbers=layout,
        preferred_element_type=jnp.float32,
    )


def group_sums(values):
    tiles = values.shape[0]
    width = values.shape[-1]
    grouped = values.reshape(tiles, -1, GROUPS, width // GROUPS)
    return (jnp.sum(grouped, axis=(1, 3)), jnp.sum(grouped * grouped, axis=(1, 3)))


def shifted(x, shift, n):
    if shift > 0:
        perm = [(i, i + shift) for i in range(n - shift)]
    else:
        perm = [(i, i + shift) for i in range(-shift, n)]
    return lax.ppermute(x, AXES, perm)


def clip_totals(clips, stats):
    n = lax.axis_size("slab") * lax.axis_size("dev")
    member = (clips[:, None] == clips[None, :]).astype(jnp.float32)
    own = jnp.dot(member, stats, precision=precise)
    clip_f = clips.astype(jnp.float32)
    to_right = jnp.concatenate([clip_f[-1:], own[-1]])[None, :]
    to_left = jnp.concatenate([clip_f[:1], own[0]])[None, :]
    received = jnp.concatenate(
        [
            shifted(to_right, 1, n),
            shifted(to_right, 2, n),
            shifted(to_left, -1, n),
            shifted(to_left, -2, n),
        ],
        axis=0,
    )
    match = (clip_f[:, None] == received[None, :, 0]).astype(jnp.float32)
    return own + jnp.dot(match, received[:, 1:], precision=precise)


def finish_stats(totals, per_tile):
    voxels = totals[:, -1:] * per_tile
    means = totals[:, :GROUPS] / voxels
    variance = totals[:, GROUPS : 2 * GROUPS] / voxels - means * means
    return (means, lax.rsqrt(variance + epsilon))


def normalize(values, means, scales, gain, offset):
    tiles = values.shape[0]
    width = values.shape[-1]
    grouped = values.astype(jnp.float32).reshape(tiles, -1, GROUPS, width // GROUPS)
    scaled = (grouped - means[:, None, :, None]) * scales[:, None, :, None]
    result = scaled.reshape(values.shape) * gain + offset
    return jax.nn.silu(result).astype(jnp.bfloat16)


def arrival_rank(targets):
    order = jnp.arange(targets.shape[0])
    earlier = (targets[None, :] == targets[:, None]) & (order[None, :] < order[:, None])
    return jnp.sum(earlier.astype(jnp.int32), axis=1)


def route(values, place, slots):
    pick = (jnp.arange(slots, dtype=jnp.int32)[:, None] == place[None, :]).astype(values.dtype)
    if values.dtype == jnp.float32:
        moved = jnp.dot(pick, values, precision=precise)
    else:
        moved = jnp.dot(pick, values, preferred_element_type=jnp.float32)
    return moved.astype(values.dtype)


def to_encoders(values, group_width, capacity):
    shape = values.shape
    moved = lax.all_to_all(
        values.reshape((group_width, capacity) + shape[1:]),
        "dev",
        split_axis=0,
        concat_axis=0,
        tiled=True,
    )
    return moved.reshape(shape)


def first_conv(tiles, conv_first):
    hidden = conv_local(tiles, conv_first, 1).astype(jnp.bfloat16)
    return hidden, group_sums(hidden.astype(jnp.float32))


def second_conv(hidden, means, scales, gain_first, bias_first, conv_down):
    active = normalize(hidden, means, scales, gain_first, bias_first)
    down = conv_local(active, conv_down, 2).astype(jnp.bfloat16)
    return down, group_sums(down.astype(jnp.float32))


def per_device(
    pixels,
    tile_clip,
    tile_encoder,
    slot_owner,
    conv_first,
    gain_first,
    bias_first,
    conv_down,
    gain_second,
    bias_second,
    project,
    project_bias,
):
    group_width = lax.axis_size("dev")
    slots = slot_owner.shape[0]
    capacity = slots // group_width
    how_many = pixels.shape[0]
    encoder = tile_encoder[:, 0]
    owner = slot_owner[:, 0]
    place = encoder * capacity + arrival_rank(encoder)
    target = owner * capacity + arrival_rank(owner)
    ones = jnp.ones((how_many, 1), jnp.float32)

    slot_pixels = to_encoders(route(pixels, place, slots), group_width, capacity)

    tiles = pixels.reshape(how_many, FR, HT, WT, 3)
    hidden, (sums, squares) = first_conv(tiles, conv_first)
    totals = clip_totals(tile_clip, jnp.concatenate([sums, squares, ones], axis=1))
    means_a, scales_a = finish_stats(totals, FR * HT * WT * (C1 // GROUPS))
    slot_a = to_encoders(
        route(jnp.concatenate([means_a, scales_a], axis=1), place, slots), group_width, capacity
    )
    down, (sums, squares) = second_conv(hidden, means_a, scales_a, gain_first, bias_first, conv_down)
    totals = clip_totals(tile_clip, jnp.concatenate([sums, squares, ones], axis=1))
    means_b, scales_b = finish_stats(totals, LROWS * (C2 // GROUPS))
    slot_b = to_encoders(
        route(jnp.concatenate([means_b, scales_b, ones], axis=1), place, slots),
        group_width,
        capacity,
    )

    slot_tiles = slot_pixels.reshape(slots, FR, HT, WT, 3)
    slot_hidden, _ = first_conv(slot_tiles, conv_first)
    slot_down, _ = second_conv(
        slot_hidden, slot_a[:, :GROUPS], slot_a[:, GROUPS:], gain_first, bias_first, conv_down
    )
    active = normalize(
        slot_down, slot_b[:, :GROUPS], slot_b[:, GROUPS : 2 * GROUPS], gain_second, bias_second
    )
    flat = active.reshape(-1, C2)
    latent = jnp.dot(flat, project, preferred_element_type=jnp.float32) + project_bias
    latent = latent.astype(jnp.bfloat16).reshape(slots, LROWS * LAT)
    live = slot_b[:, 2 * GROUPS :] > 0.5
    latent = jnp.where(live, latent, jnp.zeros_like(latent))

    forward = route(latent, target, slots)
    received = to_encoders(forward, group_width, capacity)
    return received.reshape(slots * LROWS, LAT)


def solution(mesh):
    in_specs = (
        P(AXES, None),
        P(AXES),
        P(AXES, None),
        P(AXES, None),
        P(),
        P(),
        P(),
        P(),
        P(),
        P(),
        P(),
        P(),
    )
    out_specs = P(AXES, None)
    return jax.shard_map(
        per_device, mesh=mesh, in_specs=in_specs, out_specs=out_specs, check_vma=False
    )
```

```python
import jax
import jax.numpy as jnp
from jax import lax
from jax.sharding import PartitionSpec as P

C1 = 128
C2 = 256
LAT = 128
GROUPS = 32
FR = 2
HT = 8
WT = 8
LROWS = 32
AXES = ("slab", "dev")


epsilon = 1e-05
layout = ("NDHWC", "DHWIO", "NDHWC")
precise = lax.Precision.HIGHEST


def conv_local(inputs, kernel, stride):
    return lax.conv_general_dilated(
        inputs,
        kernel,
        (1, stride, stride),
        ((2, 0), (1, 1), (1, 1)),
        dimension_numbers=layout,
        preferred_element_type=jnp.float32,
    )


def group_sums(values):
    tiles = values.shape[0]
    width = values.shape[-1]
    grouped = values.reshape(tiles, -1, GROUPS, width // GROUPS)
    return (jnp.sum(grouped, axis=(1, 3)), jnp.sum(grouped * grouped, axis=(1, 3)))


def shifted(x, shift, n):
    if shift > 0:
        perm = [(i, i + shift) for i in range(n - shift)]
    else:
        perm = [(i, i + shift) for i in range(-shift, n)]
    return lax.ppermute(x, AXES, perm)


def clip_totals(clips, stats):
    n = lax.axis_size("slab") * lax.axis_size("dev")
    member = (clips[:, None] == clips[None, :]).astype(jnp.float32)
    own = jnp.dot(member, stats, precision=precise)
    clip_f = clips.astype(jnp.float32)
    to_right = jnp.concatenate([clip_f[-1:], own[-1]])[None, :]
    to_left = jnp.concatenate([clip_f[:1], own[0]])[None, :]
    received = jnp.concatenate(
        [
            shifted(to_right, 1, n),
            shifted(to_right, 2, n),
            shifted(to_left, -1, n),
            shifted(to_left, -2, n),
        ],
        axis=0,
    )
    match = (clip_f[:, None] == received[None, :, 0]).astype(jnp.float32)
    return own + jnp.dot(match, received[:, 1:], precision=precise)


def finish_stats(totals, per_tile):
    voxels = totals[:, -1:] * per_tile
    means = totals[:, :GROUPS] / voxels
    variance = totals[:, GROUPS : 2 * GROUPS] / voxels - means * means
    return (means, lax.rsqrt(variance + epsilon))


def normalize(values, means, scales, gain, offset):
    tiles = values.shape[0]
    width = values.shape[-1]
    grouped = values.astype(jnp.float32).reshape(tiles, -1, GROUPS, width // GROUPS)
    scaled = (grouped - means[:, None, :, None]) * scales[:, None, :, None]
    result = scaled.reshape(values.shape) * gain + offset
    return jax.nn.silu(result).astype(jnp.bfloat16)


def arrival_rank(targets):
    order = jnp.arange(targets.shape[0])
    earlier = (targets[None, :] == targets[:, None]) & (order[None, :] < order[:, None])
    return jnp.sum(earlier.astype(jnp.int32), axis=1)


def route(values, place, slots):
    pick = (jnp.arange(slots, dtype=jnp.int32)[:, None] == place[None, :]).astype(values.dtype)
    return jnp.dot(pick, values, preferred_element_type=jnp.float32).astype(values.dtype)


def encode(tiles, clips, weights):
    (
        conv_first,
        gain_first,
        bias_first,
        conv_down,
        gain_second,
        bias_second,
        project,
        project_bias,
    ) = weights
    how_many = tiles.shape[0]
    ones = jnp.ones((how_many, 1), jnp.float32)

    hidden = conv_local(tiles, conv_first, 1).astype(jnp.bfloat16)
    sums, squares = group_sums(hidden.astype(jnp.float32))
    totals = clip_totals(clips, jnp.concatenate([sums, squares, ones], axis=1))
    means, scales = finish_stats(totals, FR * HT * WT * (C1 // GROUPS))
    active = normalize(hidden, means, scales, gain_first, bias_first)

    down = conv_local(active, conv_down, 2).astype(jnp.bfloat16)
    sums, squares = group_sums(down.astype(jnp.float32))
    totals = clip_totals(clips, jnp.concatenate([sums, squares, ones], axis=1))
    means, scales = finish_stats(totals, LROWS * (C2 // GROUPS))
    active = normalize(down, means, scales, gain_second, bias_second)

    flat = active.reshape(-1, C2)
    latent = jnp.dot(flat, project, preferred_element_type=jnp.float32) + project_bias
    return latent.astype(jnp.bfloat16).reshape(how_many, LROWS, LAT)


def per_device(
    pixels,
    tile_clip,
    tile_encoder,
    slot_owner,
    conv_first,
    gain_first,
    bias_first,
    conv_down,
    gain_second,
    bias_second,
    project,
    project_bias,
):
    weights = (
        conv_first,
        gain_first,
        bias_first,
        conv_down,
        gain_second,
        bias_second,
        project,
        project_bias,
    )
    group_width = lax.axis_size("dev")
    slots = slot_owner.shape[0]
    capacity = slots // group_width
    encoder = tile_encoder[:, 0]
    owner = slot_owner[:, 0]
    place = encoder * capacity + arrival_rank(encoder)
    target = owner * capacity + arrival_rank(owner)

    how_many = pixels.shape[0]
    tiles = pixels.reshape(how_many, FR, HT, WT, 3)
    latents = encode(tiles, tile_clip, weights)

    outgoing = route(latents.reshape(how_many, LROWS * LAT), place, slots)
    arrived = lax.all_to_all(
        outgoing.reshape(group_width, capacity, LROWS, LAT),
        "dev",
        split_axis=0,
        concat_axis=0,
        tiled=True,
    ).reshape(slots, LROWS, LAT)
    forward = route(arrived.reshape(slots, LROWS * LAT), target, slots)
    received = lax.all_to_all(
        forward.reshape(group_width, capacity, LROWS, LAT),
        "dev",
        split_axis=0,
        concat_axis=0,
        tiled=True,
    )
    return received.reshape(slots * LROWS, LAT)


def solution(mesh):
    in_specs = (
        P(AXES, None),
        P(AXES),
        P(AXES, None),
        P(AXES, None),
        P(),
        P(),
        P(),
        P(),
        P(),
        P(),
        P(),
        P(),
    )
    out_specs = P(AXES, None)
    return jax.shard_map(
        per_device, mesh=mesh, in_specs=in_specs, out_specs=out_specs, check_vma=False
    )
```

```python
import jax
import jax.numpy as jnp
from jax import lax
from jax.sharding import PartitionSpec as P

C1 = 128
C2 = 256
LAT = 128
GROUPS = 32
FR = 2
HT = 8
WT = 8
LROWS = 32
AXES = ("slab", "dev")


epsilon = 1e-05
layout = ("NDHWC", "DHWIO", "NDHWC")
precise = lax.Precision.HIGHEST


def conv_local(inputs, kernel, stride):
    return lax.conv_general_dilated(
        inputs,
        kernel,
        (1, stride, stride),
        ((2, 0), (1, 1), (1, 1)),
        dimension_numbers=layout,
        preferred_element_type=jnp.float32,
    )


def group_sums(values):
    tiles = values.shape[0]
    width = values.shape[-1]
    grouped = values.reshape(tiles, -1, GROUPS, width // GROUPS)
    return (jnp.sum(grouped, axis=(1, 3)), jnp.sum(grouped * grouped, axis=(1, 3)))


def shifted(x, shift, n):
    if shift > 0:
        perm = [(i, i + shift) for i in range(n - shift)]
    else:
        perm = [(i, i + shift) for i in range(-shift, n)]
    return lax.ppermute(x, AXES, perm)


def clip_totals(clips, stats):
    n = lax.axis_size("slab") * lax.axis_size("dev")
    member = (clips[:, None] == clips[None, :]).astype(jnp.float32)
    own = jnp.dot(member, stats, precision=precise)
    clip_f = clips.astype(jnp.float32)
    to_right = jnp.concatenate([clip_f[-1:], own[-1]])[None, :]
    to_left = jnp.concatenate([clip_f[:1], own[0]])[None, :]
    received = jnp.concatenate(
        [
            shifted(to_right, 1, n),
            shifted(to_right, 2, n),
            shifted(to_left, -1, n),
            shifted(to_left, -2, n),
        ],
        axis=0,
    )
    match = (clip_f[:, None] == received[None, :, 0]).astype(jnp.float32)
    return own + jnp.dot(match, received[:, 1:], precision=precise)


def finish_stats(totals, per_tile):
    voxels = totals[:, -1:] * per_tile
    means = totals[:, :GROUPS] / voxels
    variance = totals[:, GROUPS : 2 * GROUPS] / voxels - means * means
    return (means, lax.rsqrt(variance + epsilon))


def normalize(values, means, scales, gain, offset):
    tiles = values.shape[0]
    width = values.shape[-1]
    grouped = values.astype(jnp.float32).reshape(tiles, -1, GROUPS, width // GROUPS)
    scaled = (grouped - means[:, None, :, None]) * scales[:, None, :, None]
    result = scaled.reshape(values.shape) * gain + offset
    return jax.nn.silu(result).astype(jnp.bfloat16)


def arrival_rank(targets):
    order = jnp.arange(targets.shape[0])
    earlier = (targets[None, :] == targets[:, None]) & (order[None, :] < order[:, None])
    return jnp.sum(earlier.astype(jnp.int32), axis=1)


def route(values, place, slots):
    pick = (jnp.arange(slots, dtype=jnp.int32)[:, None] == place[None, :]).astype(values.dtype)
    if values.dtype == jnp.float32:
        moved = jnp.dot(pick, values, precision=precise)
    else:
        moved = jnp.dot(pick, values, preferred_element_type=jnp.float32)
    return moved.astype(values.dtype)


def to_encoders(values, group_width, capacity):
    shape = values.shape
    moved = lax.all_to_all(
        values.reshape((group_width, capacity) + shape[1:]),
        "dev",
        split_axis=0,
        concat_axis=0,
        tiled=True,
    )
    return moved.reshape(shape)


def first_conv(tiles, conv_first):
    hidden = conv_local(tiles, conv_first, 1).astype(jnp.bfloat16)
    return hidden, group_sums(hidden.astype(jnp.float32))


def second_conv(hidden, means, scales, gain_first, bias_first, conv_down):
    active = normalize(hidden, means, scales, gain_first, bias_first)
    down = conv_local(active, conv_down, 2).astype(jnp.bfloat16)
    return down, group_sums(down.astype(jnp.float32))


def per_device(
    pixels,
    tile_clip,
    tile_encoder,
    slot_owner,
    conv_first,
    gain_first,
    bias_first,
    conv_down,
    gain_second,
    bias_second,
    project,
    project_bias,
):
    group_width = lax.axis_size("dev")
    slots = slot_owner.shape[0]
    capacity = slots // group_width
    how_many = pixels.shape[0]
    encoder = tile_encoder[:, 0]
    owner = slot_owner[:, 0]
    place = encoder * capacity + arrival_rank(encoder)
    target = owner * capacity + arrival_rank(owner)
    ones = jnp.ones((how_many, 1), jnp.float32)

    slot_pixels = to_encoders(route(pixels, place, slots), group_width, capacity)

    tiles = pixels.reshape(how_many, FR, HT, WT, 3)
    hidden, (sums, squares) = first_conv(tiles, conv_first)
    totals = clip_totals(tile_clip, jnp.concatenate([sums, squares, ones], axis=1))
    slot_pixels, totals = lax.optimization_barrier((slot_pixels, totals))
    means_a, scales_a = finish_stats(totals, FR * HT * WT * (C1 // GROUPS))
    down, (sums, squares) = second_conv(hidden, means_a, scales_a, gain_first, bias_first, conv_down)
    slot_tiles = slot_pixels.reshape(slots, FR, HT, WT, 3)
    slot_hidden, _ = first_conv(slot_tiles, conv_first)
    totals = clip_totals(tile_clip, jnp.concatenate([sums, squares, ones], axis=1))
    slot_hidden, totals = lax.optimization_barrier((slot_hidden, totals))
    means_b, scales_b = finish_stats(totals, LROWS * (C2 // GROUPS))
    slot_stats = to_encoders(
        route(jnp.concatenate([means_a, scales_a, means_b, scales_b, ones], axis=1), place, slots),
        group_width,
        capacity,
    )

    g = GROUPS
    slot_down, _ = second_conv(
        slot_hidden, slot_stats[:, :g], slot_stats[:, g : 2 * g], gain_first, bias_first, conv_down
    )
    active = normalize(
        slot_down, slot_stats[:, 2 * g : 3 * g], slot_stats[:, 3 * g : 4 * g], gain_second, bias_second
    )
    flat = active.reshape(-1, C2)
    latent = jnp.dot(flat, project, preferred_element_type=jnp.float32) + project_bias
    latent = latent.astype(jnp.bfloat16).reshape(slots, LROWS * LAT)
    live = slot_stats[:, 4 * g :] > 0.5
    latent = jnp.where(live, latent, jnp.zeros_like(latent))

    forward = route(latent, target, slots)
    received = to_encoders(forward, group_width, capacity)
    return received.reshape(slots * LROWS, LAT)


def solution(mesh):
    in_specs = (
        P(AXES, None),
        P(AXES),
        P(AXES, None),
        P(AXES, None),
        P(),
        P(),
        P(),
        P(),
        P(),
        P(),
        P(),
        P(),
    )
    out_specs = P(AXES, None)
    return jax.shard_map(
        per_device, mesh=mesh, in_specs=in_specs, out_specs=out_specs, check_vma=False
    )
```

```python
import jax
import jax.numpy as jnp
from jax import lax
from jax.sharding import PartitionSpec as P

C1 = 128
C2 = 256
LAT = 128
GROUPS = 32
FR = 2
HT = 8
WT = 8
LROWS = 32
AXES = ("slab", "dev")


epsilon = 1e-05
layout = ("NDHWC", "DHWIO", "NDHWC")
precise = lax.Precision.HIGHEST


def conv_local(inputs, kernel, stride):
    return lax.conv_general_dilated(
        inputs,
        kernel,
        (1, stride, stride),
        ((2, 0), (1, 1), (1, 1)),
        dimension_numbers=layout,
        preferred_element_type=jnp.float32,
    )


def group_sums(values):
    tiles = values.shape[0]
    width = values.shape[-1]
    grouped = values.reshape(tiles, -1, GROUPS, width // GROUPS)
    return (jnp.sum(grouped, axis=(1, 3)), jnp.sum(grouped * grouped, axis=(1, 3)))


def shifted(x, shift, n):
    if shift > 0:
        perm = [(i, i + shift) for i in range(n - shift)]
    else:
        perm = [(i, i + shift) for i in range(-shift, n)]
    return lax.ppermute(x, AXES, perm)


def clip_totals(clips, stats):
    n = lax.axis_size("slab") * lax.axis_size("dev")
    member = (clips[:, None] == clips[None, :]).astype(jnp.float32)
    own = jnp.dot(member, stats, precision=precise)
    clip_f = clips.astype(jnp.float32)
    to_right = jnp.concatenate([clip_f[-1:], own[-1]])[None, :]
    to_left = jnp.concatenate([clip_f[:1], own[0]])[None, :]
    received = jnp.concatenate(
        [
            shifted(to_right, 1, n),
            shifted(to_right, 2, n),
            shifted(to_left, -1, n),
            shifted(to_left, -2, n),
        ],
        axis=0,
    )
    match = (clip_f[:, None] == received[None, :, 0]).astype(jnp.float32)
    return own + jnp.dot(match, received[:, 1:], precision=precise)


def finish_stats(totals, per_tile):
    voxels = totals[:, -1:] * per_tile
    means = totals[:, :GROUPS] / voxels
    variance = totals[:, GROUPS : 2 * GROUPS] / voxels - means * means
    return (means, lax.rsqrt(variance + epsilon))


def normalize(values, means, scales, gain, offset):
    tiles = values.shape[0]
    width = values.shape[-1]
    grouped = values.astype(jnp.float32).reshape(tiles, -1, GROUPS, width // GROUPS)
    scaled = (grouped - means[:, None, :, None]) * scales[:, None, :, None]
    result = scaled.reshape(values.shape) * gain + offset
    return jax.nn.silu(result).astype(jnp.bfloat16)


def arrival_rank(targets):
    order = jnp.arange(targets.shape[0])
    earlier = (targets[None, :] == targets[:, None]) & (order[None, :] < order[:, None])
    return jnp.sum(earlier.astype(jnp.int32), axis=1)


def route(values, place, slots):
    pick = (jnp.arange(slots, dtype=jnp.int32)[:, None] == place[None, :]).astype(values.dtype)
    return jnp.dot(pick, values, preferred_element_type=jnp.float32).astype(values.dtype)


def encode(tiles, clips, weights):
    (
        conv_first,
        gain_first,
        bias_first,
        conv_down,
        gain_second,
        bias_second,
        project,
        project_bias,
    ) = weights
    how_many = tiles.shape[0]
    ones = jnp.ones((how_many, 1), jnp.float32)

    hidden = conv_local(tiles, conv_first, 1).astype(jnp.bfloat16)
    sums, squares = group_sums(hidden.astype(jnp.float32))
    totals = clip_totals(clips, jnp.concatenate([sums, squares, ones], axis=1))
    means, scales = finish_stats(totals, FR * HT * WT * (C1 // GROUPS))
    active = normalize(hidden, means, scales, gain_first, bias_first)

    down = conv_local(active, conv_down, 2).astype(jnp.bfloat16)
    sums, squares = group_sums(down.astype(jnp.float32))
    totals = clip_totals(clips, jnp.concatenate([sums, squares, ones], axis=1))
    means, scales = finish_stats(totals, LROWS * (C2 // GROUPS))
    active = normalize(down, means, scales, gain_second, bias_second)

    flat = active.reshape(-1, C2)
    latent = jnp.dot(flat, project, preferred_element_type=jnp.float32) + project_bias
    return latent.astype(jnp.bfloat16).reshape(how_many, LROWS, LAT)


def per_device(
    pixels,
    tile_clip,
    tile_encoder,
    slot_owner,
    conv_first,
    gain_first,
    bias_first,
    conv_down,
    gain_second,
    bias_second,
    project,
    project_bias,
):
    weights = (
        conv_first,
        gain_first,
        bias_first,
        conv_down,
        gain_second,
        bias_second,
        project,
        project_bias,
    )
    group_width = lax.axis_size("dev")
    slots = slot_owner.shape[0]
    capacity = slots // group_width
    encoder = tile_encoder[:, 0]
    owner = slot_owner[:, 0]
    place = encoder * capacity + arrival_rank(encoder)
    target = owner * capacity + arrival_rank(owner)

    how_many = pixels.shape[0]
    tiles = pixels.reshape(how_many, FR, HT, WT, 3)
    latents = encode(tiles, tile_clip, weights)

    latents, target = lax.optimization_barrier((latents, target))
    outgoing = route(latents.reshape(how_many, LROWS * LAT), place, slots)
    arrived = lax.all_to_all(
        outgoing.reshape(group_width, capacity, LROWS, LAT),
        "dev",
        split_axis=0,
        concat_axis=0,
        tiled=True,
    ).reshape(slots, LROWS, LAT)
    forward = route(arrived.reshape(slots, LROWS * LAT), target, slots)
    received = lax.all_to_all(
        forward.reshape(group_width, capacity, LROWS, LAT),
        "dev",
        split_axis=0,
        concat_axis=0,
        tiled=True,
    )
    return received.reshape(slots * LROWS, LAT)


def solution(mesh):
    in_specs = (
        P(AXES, None),
        P(AXES),
        P(AXES, None),
        P(AXES, None),
        P(),
        P(),
        P(),
        P(),
        P(),
        P(),
        P(),
        P(),
    )
    out_specs = P(AXES, None)
    return jax.shard_map(
        per_device, mesh=mesh, in_specs=in_specs, out_specs=out_specs, check_vma=False
    )
```

```python
import jax
import jax.numpy as jnp
from jax import lax
from jax.sharding import PartitionSpec as P

C1 = 128
C2 = 256
LAT = 128
GROUPS = 32
FR = 2
HT = 8
WT = 8
LROWS = 32
AXES = ("slab", "dev")


epsilon = 1e-05
layout = ("NDHWC", "DHWIO", "NDHWC")
precise = lax.Precision.HIGHEST


def conv_local(inputs, kernel, stride):
    return lax.conv_general_dilated(
        inputs,
        kernel,
        (1, stride, stride),
        ((2, 0), (1, 1), (1, 1)),
        dimension_numbers=layout,
        preferred_element_type=jnp.float32,
    )


def group_sums(values):
    tiles = values.shape[0]
    width = values.shape[-1]
    grouped = values.reshape(tiles, -1, GROUPS, width // GROUPS)
    return (jnp.sum(grouped, axis=(1, 3)), jnp.sum(grouped * grouped, axis=(1, 3)))


def shifted(x, shift, n):
    if shift > 0:
        perm = [(i, i + shift) for i in range(n - shift)]
    else:
        perm = [(i, i + shift) for i in range(-shift, n)]
    return lax.ppermute(x, AXES, perm)


def clip_totals(clips, stats):
    n = lax.axis_size("slab") * lax.axis_size("dev")
    member = (clips[:, None] == clips[None, :]).astype(jnp.float32)
    own = jnp.dot(member, stats, precision=precise)
    clip_f = clips.astype(jnp.float32)
    to_right = jnp.concatenate([clip_f[-1:], own[-1]])
    to_left = jnp.concatenate([clip_f[:1], own[0]])
    mine = jnp.stack([to_left, to_right])
    partner = lax.ppermute(mine, AXES, [(i, i ^ 1) for i in range(n)])
    odd = (lax.axis_index(AXES) % 2) == 1
    pair = jnp.where(odd, jnp.concatenate([partner, mine]), jnp.concatenate([mine, partner]))
    from_left = shifted(pair, 2, n)
    from_right = shifted(pair, -2, n)
    left_near = jnp.where(odd, partner[1], from_left[3])
    left_far = jnp.where(odd, from_left[3], from_left[1])
    right_near = jnp.where(odd, from_right[0], partner[0])
    right_far = jnp.where(odd, from_right[2], from_right[0])
    received = jnp.stack([left_near, left_far, right_near, right_far])
    match = (clip_f[:, None] == received[None, :, 0]).astype(jnp.float32)
    return own + jnp.dot(match, received[:, 1:], precision=precise)


def finish_stats(totals, per_tile):
    voxels = totals[:, -1:] * per_tile
    means = totals[:, :GROUPS] / voxels
    variance = totals[:, GROUPS : 2 * GROUPS] / voxels - means * means
    return (means, lax.rsqrt(variance + epsilon))


def normalize(values, means, scales, gain, offset):
    tiles = values.shape[0]
    width = values.shape[-1]
    grouped = values.astype(jnp.float32).reshape(tiles, -1, GROUPS, width // GROUPS)
    scaled = (grouped - means[:, None, :, None]) * scales[:, None, :, None]
    result = scaled.reshape(values.shape) * gain + offset
    return jax.nn.silu(result).astype(jnp.bfloat16)


def arrival_rank(targets):
    order = jnp.arange(targets.shape[0])
    earlier = (targets[None, :] == targets[:, None]) & (order[None, :] < order[:, None])
    return jnp.sum(earlier.astype(jnp.int32), axis=1)


def route(values, place, slots):
    pick = (jnp.arange(slots, dtype=jnp.int32)[:, None] == place[None, :]).astype(values.dtype)
    return jnp.dot(pick, values, preferred_element_type=jnp.float32).astype(values.dtype)


def encode(tiles, clips, weights):
    (
        conv_first,
        gain_first,
        bias_first,
        conv_down,
        gain_second,
        bias_second,
        project,
        project_bias,
    ) = weights
    how_many = tiles.shape[0]
    ones = jnp.ones((how_many, 1), jnp.float32)

    hidden = conv_local(tiles, conv_first, 1).astype(jnp.bfloat16)
    sums, squares = group_sums(hidden.astype(jnp.float32))
    totals = clip_totals(clips, jnp.concatenate([sums, squares, ones], axis=1))
    means, scales = finish_stats(totals, FR * HT * WT * (C1 // GROUPS))
    active = normalize(hidden, means, scales, gain_first, bias_first)

    down = conv_local(active, conv_down, 2).astype(jnp.bfloat16)
    sums, squares = group_sums(down.astype(jnp.float32))
    totals = clip_totals(clips, jnp.concatenate([sums, squares, ones], axis=1))
    means, scales = finish_stats(totals, LROWS * (C2 // GROUPS))
    active = normalize(down, means, scales, gain_second, bias_second)

    flat = active.reshape(-1, C2)
    latent = jnp.dot(flat, project, preferred_element_type=jnp.float32) + project_bias
    return latent.astype(jnp.bfloat16).reshape(how_many, LROWS, LAT)


def per_device(
    pixels,
    tile_clip,
    tile_encoder,
    slot_owner,
    conv_first,
    gain_first,
    bias_first,
    conv_down,
    gain_second,
    bias_second,
    project,
    project_bias,
):
    weights = (
        conv_first,
        gain_first,
        bias_first,
        conv_down,
        gain_second,
        bias_second,
        project,
        project_bias,
    )
    group_width = lax.axis_size("dev")
    slots = slot_owner.shape[0]
    capacity = slots // group_width
    encoder = tile_encoder[:, 0]
    owner = slot_owner[:, 0]
    place = encoder * capacity + arrival_rank(encoder)
    target = owner * capacity + arrival_rank(owner)

    how_many = pixels.shape[0]
    tiles = pixels.reshape(how_many, FR, HT, WT, 3)
    latents = encode(tiles, tile_clip, weights)

    latents, target = lax.optimization_barrier((latents, target))
    outgoing = route(latents.reshape(how_many, LROWS * LAT), place, slots)
    arrived = lax.all_to_all(
        outgoing.reshape(group_width, capacity, LROWS, LAT),
        "dev",
        split_axis=0,
        concat_axis=0,
        tiled=True,
    ).reshape(slots, LROWS, LAT)
    forward = route(arrived.reshape(slots, LROWS * LAT), target, slots)
    received = lax.all_to_all(
        forward.reshape(group_width, capacity, LROWS, LAT),
        "dev",
        split_axis=0,
        concat_axis=0,
        tiled=True,
    )
    return received.reshape(slots * LROWS, LAT)


def solution(mesh):
    in_specs = (
        P(AXES, None),
        P(AXES),
        P(AXES, None),
        P(AXES, None),
        P(),
        P(),
        P(),
        P(),
        P(),
        P(),
        P(),
        P(),
    )
    out_specs = P(AXES, None)
    return jax.shard_map(
        per_device, mesh=mesh, in_specs=in_specs, out_specs=out_specs, check_vma=False
    )
```

```python
import jax
import jax.numpy as jnp
from jax import lax
from jax.sharding import PartitionSpec as P

C1 = 128
C2 = 256
LAT = 128
GROUPS = 32
FR = 2
HT = 8
WT = 8
LROWS = 32
AXES = ("slab", "dev")


epsilon = 1e-05
layout = ("NDHWC", "DHWIO", "NDHWC")
precise = lax.Precision.HIGHEST


def conv_local(inputs, kernel, stride):
    return lax.conv_general_dilated(
        inputs,
        kernel,
        (1, stride, stride),
        ((2, 0), (1, 1), (1, 1)),
        dimension_numbers=layout,
        preferred_element_type=jnp.float32,
    )


def group_sums(values):
    tiles = values.shape[0]
    width = values.shape[-1]
    grouped = values.reshape(tiles, -1, GROUPS, width // GROUPS)
    return (jnp.sum(grouped, axis=(1, 3)), jnp.sum(grouped * grouped, axis=(1, 3)))


def shifted(x, shift, n):
    if shift > 0:
        perm = [(i, i + shift) for i in range(n - shift)]
    else:
        perm = [(i, i + shift) for i in range(-shift, n)]
    return lax.ppermute(x, AXES, perm)


def clip_totals(clips, stats):
    n = lax.axis_size("slab") * lax.axis_size("dev")
    ends = jnp.stack([clips[0], clips[-1]])
    edge = (ends[:, None] == clips[None, :]).astype(jnp.float32)
    edge_sums = jnp.dot(edge, stats, precision=precise)
    mine = jnp.concatenate([ends.astype(jnp.float32)[:, None], edge_sums], axis=1)
    clip_f = clips.astype(jnp.float32)
    partner = lax.ppermute(mine, AXES, [(i, i ^ 1) for i in range(n)])
    odd = (lax.axis_index(AXES) % 2) == 1
    pair = jnp.where(odd, jnp.concatenate([partner, mine]), jnp.concatenate([mine, partner]))
    from_left = shifted(pair, 2, n)
    from_right = shifted(pair, -2, n)
    left_near = jnp.where(odd, partner[1], from_left[3])
    left_far = jnp.where(odd, from_left[3], from_left[1])
    right_near = jnp.where(odd, from_right[0], partner[0])
    right_far = jnp.where(odd, from_right[2], from_right[0])
    received = jnp.stack([left_near, left_far, right_near, right_far])
    member = (clips[:, None] == clips[None, :]).astype(jnp.float32)
    own = jnp.dot(member, stats, precision=precise)
    match = (clip_f[:, None] == received[None, :, 0]).astype(jnp.float32)
    return own + jnp.dot(match, received[:, 1:], precision=precise)


def finish_stats(totals, per_tile):
    voxels = totals[:, -1:] * per_tile
    means = totals[:, :GROUPS] / voxels
    variance = totals[:, GROUPS : 2 * GROUPS] / voxels - means * means
    return (means, lax.rsqrt(variance + epsilon))


def normalize(values, means, scales, gain, offset):
    tiles = values.shape[0]
    width = values.shape[-1]
    grouped = values.astype(jnp.float32).reshape(tiles, -1, GROUPS, width // GROUPS)
    scaled = (grouped - means[:, None, :, None]) * scales[:, None, :, None]
    result = scaled.reshape(values.shape) * gain + offset
    return jax.nn.silu(result).astype(jnp.bfloat16)


def arrival_rank(targets):
    order = jnp.arange(targets.shape[0])
    earlier = (targets[None, :] == targets[:, None]) & (order[None, :] < order[:, None])
    return jnp.sum(earlier.astype(jnp.int32), axis=1)


def route(values, place, slots):
    pick = (jnp.arange(slots, dtype=jnp.int32)[:, None] == place[None, :]).astype(values.dtype)
    return jnp.dot(pick, values, preferred_element_type=jnp.float32).astype(values.dtype)


def encode(tiles, clips, weights):
    (
        conv_first,
        gain_first,
        bias_first,
        conv_down,
        gain_second,
        bias_second,
        project,
        project_bias,
    ) = weights
    how_many = tiles.shape[0]
    ones = jnp.ones((how_many, 1), jnp.float32)

    hidden = conv_local(tiles, conv_first, 1).astype(jnp.bfloat16)
    sums, squares = group_sums(hidden.astype(jnp.float32))
    totals = clip_totals(clips, jnp.concatenate([sums, squares, ones], axis=1))
    means, scales = finish_stats(totals, FR * HT * WT * (C1 // GROUPS))
    active = normalize(hidden, means, scales, gain_first, bias_first)

    down = conv_local(active, conv_down, 2).astype(jnp.bfloat16)
    sums, squares = group_sums(down.astype(jnp.float32))
    totals = clip_totals(clips, jnp.concatenate([sums, squares, ones], axis=1))
    means, scales = finish_stats(totals, LROWS * (C2 // GROUPS))
    active = normalize(down, means, scales, gain_second, bias_second)

    flat = active.reshape(-1, C2)
    latent = jnp.dot(flat, project, preferred_element_type=jnp.float32) + project_bias
    return latent.astype(jnp.bfloat16).reshape(how_many, LROWS, LAT)


def per_device(
    pixels,
    tile_clip,
    tile_encoder,
    slot_owner,
    conv_first,
    gain_first,
    bias_first,
    conv_down,
    gain_second,
    bias_second,
    project,
    project_bias,
):
    weights = (
        conv_first,
        gain_first,
        bias_first,
        conv_down,
        gain_second,
        bias_second,
        project,
        project_bias,
    )
    group_width = lax.axis_size("dev")
    slots = slot_owner.shape[0]
    capacity = slots // group_width
    encoder = tile_encoder[:, 0]
    owner = slot_owner[:, 0]
    place = encoder * capacity + arrival_rank(encoder)
    target = owner * capacity + arrival_rank(owner)

    how_many = pixels.shape[0]
    tiles = pixels.reshape(how_many, FR, HT, WT, 3)
    latents = encode(tiles, tile_clip, weights)

    latents, target = lax.optimization_barrier((latents, target))
    outgoing = route(latents.reshape(how_many, LROWS * LAT), place, slots)
    arrived = lax.all_to_all(
        outgoing.reshape(group_width, capacity, LROWS, LAT),
        "dev",
        split_axis=0,
        concat_axis=0,
        tiled=True,
    ).reshape(slots, LROWS, LAT)
    forward = route(arrived.reshape(slots, LROWS * LAT), target, slots)
    received = lax.all_to_all(
        forward.reshape(group_width, capacity, LROWS, LAT),
        "dev",
        split_axis=0,
        concat_axis=0,
        tiled=True,
    )
    return received.reshape(slots * LROWS, LAT)


def solution(mesh):
    in_specs = (
        P(AXES, None),
        P(AXES),
        P(AXES, None),
        P(AXES, None),
        P(),
        P(),
        P(),
        P(),
        P(),
        P(),
        P(),
        P(),
    )
    out_specs = P(AXES, None)
    return jax.shard_map(
        per_device, mesh=mesh, in_specs=in_specs, out_specs=out_specs, check_vma=False
    )
```

```python
import jax
import jax.numpy as jnp
from jax import lax
from jax.sharding import PartitionSpec as P

C1 = 128
C2 = 256
LAT = 128
GROUPS = 32
FR = 2
HT = 8
WT = 8
LROWS = 32
AXES = ("slab", "dev")


epsilon = 1e-05
layout = ("NDHWC", "DHWIO", "NDHWC")
precise = lax.Precision.HIGHEST


def conv_local(inputs, kernel, stride):
    return lax.conv_general_dilated(
        inputs,
        kernel,
        (1, stride, stride),
        ((2, 0), (1, 1), (1, 1)),
        dimension_numbers=layout,
        preferred_element_type=jnp.float32,
    )


def group_sums(values):
    tiles = values.shape[0]
    width = values.shape[-1]
    grouped = values.reshape(tiles, -1, GROUPS, width // GROUPS)
    return (jnp.sum(grouped, axis=(1, 3)), jnp.sum(grouped * grouped, axis=(1, 3)))


def shifted(x, shift, n):
    if shift > 0:
        perm = [(i, i + shift) for i in range(n - shift)]
    else:
        perm = [(i, i + shift) for i in range(-shift, n)]
    return lax.ppermute(x, AXES, perm)


def clip_totals(clips, stats):
    n = lax.axis_size("slab") * lax.axis_size("dev")
    member = (clips[:, None] == clips[None, :]).astype(jnp.float32)
    own = jnp.dot(member, stats, precision=precise)
    clip_f = clips.astype(jnp.float32)
    to_right = jnp.concatenate([clip_f[-1:], own[-1]])
    to_left = jnp.concatenate([clip_f[:1], own[0]])
    mine = jnp.stack([to_left, to_right])
    from_left = shifted(mine, 2, n)
    from_right = shifted(mine, -2, n)
    bundle = jnp.concatenate([mine, from_left, from_right])
    partner = lax.ppermute(bundle, AXES, [(i, i ^ 1) for i in range(n)])
    odd = (lax.axis_index(AXES) % 2) == 1
    left_near = jnp.where(odd, partner[1], partner[3])
    left_far = from_left[1]
    right_near = jnp.where(odd, partner[4], partner[0])
    right_far = from_right[0]
    received = jnp.stack([left_near, left_far, right_near, right_far])
    match = (clip_f[:, None] == received[None, :, 0]).astype(jnp.float32)
    return own + jnp.dot(match, received[:, 1:], precision=precise)


def finish_stats(totals, per_tile):
    voxels = totals[:, -1:] * per_tile
    means = totals[:, :GROUPS] / voxels
    variance = totals[:, GROUPS : 2 * GROUPS] / voxels - means * means
    return (means, lax.rsqrt(variance + epsilon))


def normalize(values, means, scales, gain, offset):
    tiles = values.shape[0]
    width = values.shape[-1]
    grouped = values.astype(jnp.float32).reshape(tiles, -1, GROUPS, width // GROUPS)
    scaled = (grouped - means[:, None, :, None]) * scales[:, None, :, None]
    result = scaled.reshape(values.shape) * gain + offset
    return jax.nn.silu(result).astype(jnp.bfloat16)


def arrival_rank(targets):
    order = jnp.arange(targets.shape[0])
    earlier = (targets[None, :] == targets[:, None]) & (order[None, :] < order[:, None])
    return jnp.sum(earlier.astype(jnp.int32), axis=1)


def route(values, place, slots):
    pick = (jnp.arange(slots, dtype=jnp.int32)[:, None] == place[None, :]).astype(values.dtype)
    return jnp.dot(pick, values, preferred_element_type=jnp.float32).astype(values.dtype)


def encode(tiles, clips, weights):
    (
        conv_first,
        gain_first,
        bias_first,
        conv_down,
        gain_second,
        bias_second,
        project,
        project_bias,
    ) = weights
    how_many = tiles.shape[0]
    ones = jnp.ones((how_many, 1), jnp.float32)

    hidden = conv_local(tiles, conv_first, 1).astype(jnp.bfloat16)
    sums, squares = group_sums(hidden.astype(jnp.float32))
    totals = clip_totals(clips, jnp.concatenate([sums, squares, ones], axis=1))
    means, scales = finish_stats(totals, FR * HT * WT * (C1 // GROUPS))
    active = normalize(hidden, means, scales, gain_first, bias_first)

    down = conv_local(active, conv_down, 2).astype(jnp.bfloat16)
    sums, squares = group_sums(down.astype(jnp.float32))
    totals = clip_totals(clips, jnp.concatenate([sums, squares, ones], axis=1))
    means, scales = finish_stats(totals, LROWS * (C2 // GROUPS))
    active = normalize(down, means, scales, gain_second, bias_second)

    flat = active.reshape(-1, C2)
    latent = jnp.dot(flat, project, preferred_element_type=jnp.float32) + project_bias
    return latent.astype(jnp.bfloat16).reshape(how_many, LROWS, LAT)


def per_device(
    pixels,
    tile_clip,
    tile_encoder,
    slot_owner,
    conv_first,
    gain_first,
    bias_first,
    conv_down,
    gain_second,
    bias_second,
    project,
    project_bias,
):
    weights = (
        conv_first,
        gain_first,
        bias_first,
        conv_down,
        gain_second,
        bias_second,
        project,
        project_bias,
    )
    group_width = lax.axis_size("dev")
    slots = slot_owner.shape[0]
    capacity = slots // group_width
    encoder = tile_encoder[:, 0]
    owner = slot_owner[:, 0]
    place = encoder * capacity + arrival_rank(encoder)
    target = owner * capacity + arrival_rank(owner)

    how_many = pixels.shape[0]
    tiles = pixels.reshape(how_many, FR, HT, WT, 3)
    latents = encode(tiles, tile_clip, weights)

    latents, target = lax.optimization_barrier((latents, target))
    outgoing = route(latents.reshape(how_many, LROWS * LAT), place, slots)
    arrived = lax.all_to_all(
        outgoing.reshape(group_width, capacity, LROWS, LAT),
        "dev",
        split_axis=0,
        concat_axis=0,
        tiled=True,
    ).reshape(slots, LROWS, LAT)
    forward = route(arrived.reshape(slots, LROWS * LAT), target, slots)
    received = lax.all_to_all(
        forward.reshape(group_width, capacity, LROWS, LAT),
        "dev",
        split_axis=0,
        concat_axis=0,
        tiled=True,
    )
    return received.reshape(slots * LROWS, LAT)


def solution(mesh):
    in_specs = (
        P(AXES, None),
        P(AXES),
        P(AXES, None),
        P(AXES, None),
        P(),
        P(),
        P(),
        P(),
        P(),
        P(),
        P(),
        P(),
    )
    out_specs = P(AXES, None)
    return jax.shard_map(
        per_device, mesh=mesh, in_specs=in_specs, out_specs=out_specs, check_vma=False
    )
```

```python
import jax
import jax.numpy as jnp
from jax import lax
from jax.sharding import PartitionSpec as P

C1 = 128
C2 = 256
LAT = 128
GROUPS = 32
FR = 2
HT = 8
WT = 8
LROWS = 32
AXES = ("slab", "dev")


epsilon = 1e-05
layout = ("NDHWC", "DHWIO", "NDHWC")
precise = lax.Precision.HIGHEST


def conv_local(inputs, kernel, stride):
    return lax.conv_general_dilated(
        inputs,
        kernel,
        (1, stride, stride),
        ((2, 0), (1, 1), (1, 1)),
        dimension_numbers=layout,
        preferred_element_type=jnp.float32,
    )


def group_sums(values):
    tiles = values.shape[0]
    width = values.shape[-1]
    grouped = values.reshape(tiles, -1, GROUPS, width // GROUPS)
    return (jnp.sum(grouped, axis=(1, 3)), jnp.sum(grouped * grouped, axis=(1, 3)))


def shifted(x, shift, n):
    if shift > 0:
        perm = [(i, i + shift) for i in range(n - shift)]
    else:
        perm = [(i, i + shift) for i in range(-shift, n)]
    return lax.ppermute(x, AXES, perm)


def clip_totals(clips, stats):
    n = lax.axis_size("slab") * lax.axis_size("dev")
    clip_f = clips.astype(jnp.float32)
    first = jnp.sum(jnp.where((clips == clips[0])[:, None], stats, 0.0), axis=0)
    last = jnp.sum(jnp.where((clips == clips[-1])[:, None], stats, 0.0), axis=0)
    to_right = jnp.concatenate([clip_f[-1:], last])
    to_left = jnp.concatenate([clip_f[:1], first])
    mine = jnp.stack([to_left, to_right])
    from_left = shifted(mine, 2, n)
    from_right = shifted(mine, -2, n)
    bundle = jnp.concatenate([mine, from_left, from_right])
    partner = lax.ppermute(bundle, AXES, [(i, i ^ 1) for i in range(n)])
    odd = (lax.axis_index(AXES) % 2) == 1
    left_near = jnp.where(odd, partner[1], partner[3])
    left_far = from_left[1]
    right_near = jnp.where(odd, partner[4], partner[0])
    right_far = from_right[0]
    received = jnp.stack([left_near, left_far, right_near, right_far])
    member = (clips[:, None] == clips[None, :]).astype(jnp.float32)
    own = jnp.dot(member, stats, precision=precise)
    match = (clip_f[:, None] == received[None, :, 0]).astype(jnp.float32)
    return own + jnp.dot(match, received[:, 1:], precision=precise)


def finish_stats(totals, per_tile):
    voxels = totals[:, -1:] * per_tile
    means = totals[:, :GROUPS] / voxels
    variance = totals[:, GROUPS : 2 * GROUPS] / voxels - means * means
    return (means, lax.rsqrt(variance + epsilon))


def normalize(values, means, scales, gain, offset):
    tiles = values.shape[0]
    width = values.shape[-1]
    grouped = values.astype(jnp.float32).reshape(tiles, -1, GROUPS, width // GROUPS)
    scaled = (grouped - means[:, None, :, None]) * scales[:, None, :, None]
    result = scaled.reshape(values.shape) * gain + offset
    return jax.nn.silu(result).astype(jnp.bfloat16)


def arrival_rank(targets):
    order = jnp.arange(targets.shape[0])
    earlier = (targets[None, :] == targets[:, None]) & (order[None, :] < order[:, None])
    return jnp.sum(earlier.astype(jnp.int32), axis=1)


def route(values, place, slots):
    pick = (jnp.arange(slots, dtype=jnp.int32)[:, None] == place[None, :]).astype(values.dtype)
    return jnp.dot(pick, values, preferred_element_type=jnp.float32).astype(values.dtype)


def encode(tiles, clips, weights):
    (
        conv_first,
        gain_first,
        bias_first,
        conv_down,
        gain_second,
        bias_second,
        project,
        project_bias,
    ) = weights
    how_many = tiles.shape[0]
    ones = jnp.ones((how_many, 1), jnp.float32)

    hidden = conv_local(tiles, conv_first, 1).astype(jnp.bfloat16)
    sums, squares = group_sums(hidden.astype(jnp.float32))
    totals = clip_totals(clips, jnp.concatenate([sums, squares, ones], axis=1))
    means, scales = finish_stats(totals, FR * HT * WT * (C1 // GROUPS))
    active = normalize(hidden, means, scales, gain_first, bias_first)

    down = conv_local(active, conv_down, 2).astype(jnp.bfloat16)
    sums, squares = group_sums(down.astype(jnp.float32))
    totals = clip_totals(clips, jnp.concatenate([sums, squares, ones], axis=1))
    means, scales = finish_stats(totals, LROWS * (C2 // GROUPS))
    active = normalize(down, means, scales, gain_second, bias_second)

    flat = active.reshape(-1, C2)
    latent = jnp.dot(flat, project, preferred_element_type=jnp.float32) + project_bias
    return latent.astype(jnp.bfloat16).reshape(how_many, LROWS, LAT)


def per_device(
    pixels,
    tile_clip,
    tile_encoder,
    slot_owner,
    conv_first,
    gain_first,
    bias_first,
    conv_down,
    gain_second,
    bias_second,
    project,
    project_bias,
):
    weights = (
        conv_first,
        gain_first,
        bias_first,
        conv_down,
        gain_second,
        bias_second,
        project,
        project_bias,
    )
    group_width = lax.axis_size("dev")
    slots = slot_owner.shape[0]
    capacity = slots // group_width
    encoder = tile_encoder[:, 0]
    owner = slot_owner[:, 0]
    place = encoder * capacity + arrival_rank(encoder)
    target = owner * capacity + arrival_rank(owner)

    how_many = pixels.shape[0]
    tiles = pixels.reshape(how_many, FR, HT, WT, 3)
    latents = encode(tiles, tile_clip, weights)

    latents, target = lax.optimization_barrier((latents, target))
    outgoing = route(latents.reshape(how_many, LROWS * LAT), place, slots)
    arrived = lax.all_to_all(
        outgoing.reshape(group_width, capacity, LROWS, LAT),
        "dev",
        split_axis=0,
        concat_axis=0,
        tiled=True,
    ).reshape(slots, LROWS, LAT)
    forward = route(arrived.reshape(slots, LROWS * LAT), target, slots)
    received = lax.all_to_all(
        forward.reshape(group_width, capacity, LROWS, LAT),
        "dev",
        split_axis=0,
        concat_axis=0,
        tiled=True,
    )
    return received.reshape(slots * LROWS, LAT)


def solution(mesh):
    in_specs = (
        P(AXES, None),
        P(AXES),
        P(AXES, None),
        P(AXES, None),
        P(),
        P(),
        P(),
        P(),
        P(),
        P(),
        P(),
        P(),
    )
    out_specs = P(AXES, None)
    return jax.shard_map(
        per_device, mesh=mesh, in_specs=in_specs, out_specs=out_specs, check_vma=False
    )
```

```python
import jax
import jax.numpy as jnp
from jax import lax
from jax.sharding import PartitionSpec as P

C1 = 128
C2 = 256
LAT = 128
GROUPS = 32
FR = 2
HT = 8
WT = 8
LROWS = 32
AXES = ("slab", "dev")


epsilon = 1e-05
layout = ("NDHWC", "DHWIO", "NDHWC")
precise = lax.Precision.HIGHEST


def conv_local(inputs, kernel, stride):
    return lax.conv_general_dilated(
        inputs,
        kernel,
        (1, stride, stride),
        ((2, 0), (1, 1), (1, 1)),
        dimension_numbers=layout,
        preferred_element_type=jnp.float32,
    )


def group_sums(values):
    tiles = values.shape[0]
    width = values.shape[-1]
    grouped = values.reshape(tiles, -1, GROUPS, width // GROUPS)
    return (jnp.sum(grouped, axis=(1, 3)), jnp.sum(grouped * grouped, axis=(1, 3)))


def shifted(x, shift, n):
    if shift > 0:
        perm = [(i, i + shift) for i in range(n - shift)]
    else:
        perm = [(i, i + shift) for i in range(-shift, n)]
    return lax.ppermute(x, AXES, perm)


def clip_totals(clips, stats):
    n = lax.axis_size("slab") * lax.axis_size("dev")
    member = (clips[:, None] == clips[None, :]).astype(jnp.float32)
    own = jnp.dot(member, stats, precision=precise)
    clip_f = clips.astype(jnp.float32)
    to_right = jnp.concatenate([clip_f[-1:], own[-1]])
    to_left = jnp.concatenate([clip_f[:1], own[0]])
    mine = jnp.stack([to_left, to_right])
    odd = (lax.axis_index(AXES) % 2) == 1
    partner = lax.ppermute(mine, AXES, [(i, i ^ 1) for i in range(n)])
    cross_pairs = [(i, i + 1) for i in range(1, n - 1, 2)] + [(i, i - 1) for i in range(2, n, 2)]
    across = lax.ppermute(mine, AXES, cross_pairs)
    from_left = shifted(mine, 2, n)
    from_right = shifted(mine, -2, n)
    left_near = jnp.where(odd, partner[1], across[1])
    left_far = from_left[1]
    right_near = jnp.where(odd, across[0], partner[0])
    right_far = from_right[0]
    received = jnp.stack([left_near, left_far, right_near, right_far])
    match = (clip_f[:, None] == received[None, :, 0]).astype(jnp.float32)
    return own + jnp.dot(match, received[:, 1:], precision=precise)


def finish_stats(totals, per_tile):
    voxels = totals[:, -1:] * per_tile
    means = totals[:, :GROUPS] / voxels
    variance = totals[:, GROUPS : 2 * GROUPS] / voxels - means * means
    return (means, lax.rsqrt(variance + epsilon))


def normalize(values, means, scales, gain, offset):
    tiles = values.shape[0]
    width = values.shape[-1]
    grouped = values.astype(jnp.float32).reshape(tiles, -1, GROUPS, width // GROUPS)
    scaled = (grouped - means[:, None, :, None]) * scales[:, None, :, None]
    result = scaled.reshape(values.shape) * gain + offset
    return jax.nn.silu(result).astype(jnp.bfloat16)


def arrival_rank(targets):
    order = jnp.arange(targets.shape[0])
    earlier = (targets[None, :] == targets[:, None]) & (order[None, :] < order[:, None])
    return jnp.sum(earlier.astype(jnp.int32), axis=1)


def route(values, place, slots):
    pick = (jnp.arange(slots, dtype=jnp.int32)[:, None] == place[None, :]).astype(values.dtype)
    return jnp.dot(pick, values, preferred_element_type=jnp.float32).astype(values.dtype)


def encode(tiles, clips, weights):
    (
        conv_first,
        gain_first,
        bias_first,
        conv_down,
        gain_second,
        bias_second,
        project,
        project_bias,
    ) = weights
    how_many = tiles.shape[0]
    ones = jnp.ones((how_many, 1), jnp.float32)

    hidden = conv_local(tiles, conv_first, 1).astype(jnp.bfloat16)
    sums, squares = group_sums(hidden.astype(jnp.float32))
    totals = clip_totals(clips, jnp.concatenate([sums, squares, ones], axis=1))
    means, scales = finish_stats(totals, FR * HT * WT * (C1 // GROUPS))
    active = normalize(hidden, means, scales, gain_first, bias_first)

    down = conv_local(active, conv_down, 2).astype(jnp.bfloat16)
    sums, squares = group_sums(down.astype(jnp.float32))
    totals = clip_totals(clips, jnp.concatenate([sums, squares, ones], axis=1))
    means, scales = finish_stats(totals, LROWS * (C2 // GROUPS))
    active = normalize(down, means, scales, gain_second, bias_second)

    flat = active.reshape(-1, C2)
    latent = jnp.dot(flat, project, preferred_element_type=jnp.float32) + project_bias
    return latent.astype(jnp.bfloat16).reshape(how_many, LROWS, LAT)


def per_device(
    pixels,
    tile_clip,
    tile_encoder,
    slot_owner,
    conv_first,
    gain_first,
    bias_first,
    conv_down,
    gain_second,
    bias_second,
    project,
    project_bias,
):
    weights = (
        conv_first,
        gain_first,
        bias_first,
        conv_down,
        gain_second,
        bias_second,
        project,
        project_bias,
    )
    group_width = lax.axis_size("dev")
    slots = slot_owner.shape[0]
    capacity = slots // group_width
    encoder = tile_encoder[:, 0]
    owner = slot_owner[:, 0]
    place = encoder * capacity + arrival_rank(encoder)
    target = owner * capacity + arrival_rank(owner)

    how_many = pixels.shape[0]
    tiles = pixels.reshape(how_many, FR, HT, WT, 3)
    latents = encode(tiles, tile_clip, weights)

    latents, target = lax.optimization_barrier((latents, target))
    outgoing = route(latents.reshape(how_many, LROWS * LAT), place, slots)
    arrived = lax.all_to_all(
        outgoing.reshape(group_width, capacity, LROWS, LAT),
        "dev",
        split_axis=0,
        concat_axis=0,
        tiled=True,
    ).reshape(slots, LROWS, LAT)
    forward = route(arrived.reshape(slots, LROWS * LAT), target, slots)
    received = lax.all_to_all(
        forward.reshape(group_width, capacity, LROWS, LAT),
        "dev",
        split_axis=0,
        concat_axis=0,
        tiled=True,
    )
    return received.reshape(slots * LROWS, LAT)


def solution(mesh):
    in_specs = (
        P(AXES, None),
        P(AXES),
        P(AXES, None),
        P(AXES, None),
        P(),
        P(),
        P(),
        P(),
        P(),
        P(),
        P(),
        P(),
    )
    out_specs = P(AXES, None)
    return jax.shard_map(
        per_device, mesh=mesh, in_specs=in_specs, out_specs=out_specs, check_vma=False
    )
```

```python
import jax
import jax.numpy as jnp
from jax import lax
from jax.sharding import PartitionSpec as P

C1 = 128
C2 = 256
LAT = 128
GROUPS = 32
FR = 2
HT = 8
WT = 8
LROWS = 32
AXES = ("slab", "dev")


epsilon = 1e-05
layout = ("NDHWC", "DHWIO", "NDHWC")
precise = lax.Precision.HIGHEST


def conv_local(inputs, kernel, stride):
    return lax.conv_general_dilated(
        inputs,
        kernel,
        (1, stride, stride),
        ((2, 0), (1, 1), (1, 1)),
        dimension_numbers=layout,
        preferred_element_type=jnp.float32,
    )


def group_sums(values):
    tiles = values.shape[0]
    width = values.shape[-1]
    grouped = values.reshape(tiles, -1, GROUPS, width // GROUPS)
    return (jnp.sum(grouped, axis=(1, 3)), jnp.sum(grouped * grouped, axis=(1, 3)))


def shifted(x, shift, n):
    if shift > 0:
        perm = [(i, i + shift) for i in range(n - shift)]
    else:
        perm = [(i, i + shift) for i in range(-shift, n)]
    return lax.ppermute(x, AXES, perm)


def clip_totals(clips, stats):
    n = lax.axis_size("slab") * lax.axis_size("dev")
    member = (clips[:, None] == clips[None, :]).astype(jnp.float32)
    own = jnp.dot(member, stats, precision=precise)
    clip_f = clips.astype(jnp.float32)
    to_right = jnp.concatenate([clip_f[-1:], own[-1]])
    to_left = jnp.concatenate([clip_f[:1], own[0]])
    mine = jnp.stack([to_left, to_right])
    from_left = shifted(mine, 2, n)
    from_right = shifted(mine, -2, n)
    bundle = jnp.concatenate([mine, from_left, from_right])
    partner = lax.ppermute(bundle, AXES, [(i, i ^ 1) for i in range(n)])
    odd = (lax.axis_index(AXES) % 2) == 1
    left_near = jnp.where(odd, partner[1], partner[3])
    left_far = from_left[1]
    right_near = jnp.where(odd, partner[4], partner[0])
    right_far = from_right[0]
    received = jnp.stack([left_near, left_far, right_near, right_far])
    match = (clip_f[:, None] == received[None, :, 0]).astype(jnp.float32)
    return own + jnp.dot(match, received[:, 1:], precision=precise)


def finish_stats(totals, counts, per_tile):
    voxels = counts * per_tile
    means = totals[:, :GROUPS] / voxels
    variance = totals[:, GROUPS : 2 * GROUPS] / voxels - means * means
    return (means, lax.rsqrt(variance + epsilon))


def normalize(values, means, scales, gain, offset):
    tiles = values.shape[0]
    width = values.shape[-1]
    grouped = values.astype(jnp.float32).reshape(tiles, -1, GROUPS, width // GROUPS)
    scaled = (grouped - means[:, None, :, None]) * scales[:, None, :, None]
    result = scaled.reshape(values.shape) * gain + offset
    return jax.nn.silu(result).astype(jnp.bfloat16)


def arrival_rank(targets):
    order = jnp.arange(targets.shape[0])
    earlier = (targets[None, :] == targets[:, None]) & (order[None, :] < order[:, None])
    return jnp.sum(earlier.astype(jnp.int32), axis=1)


def route(values, place, slots):
    pick = (jnp.arange(slots, dtype=jnp.int32)[:, None] == place[None, :]).astype(values.dtype)
    return jnp.dot(pick, values, preferred_element_type=jnp.float32).astype(values.dtype)


def encode(tiles, clips, weights):
    (
        conv_first,
        gain_first,
        bias_first,
        conv_down,
        gain_second,
        bias_second,
        project,
        project_bias,
    ) = weights
    how_many = tiles.shape[0]
    ones = jnp.ones((how_many, 1), jnp.float32)

    hidden = conv_local(tiles, conv_first, 1).astype(jnp.bfloat16)
    sums, squares = group_sums(hidden.astype(jnp.float32))
    totals = clip_totals(clips, jnp.concatenate([sums, squares, ones], axis=1))
    counts = totals[:, -1:]
    means, scales = finish_stats(totals, counts, FR * HT * WT * (C1 // GROUPS))
    active = normalize(hidden, means, scales, gain_first, bias_first)

    down = conv_local(active, conv_down, 2).astype(jnp.bfloat16)
    sums, squares = group_sums(down.astype(jnp.float32))
    totals = clip_totals(clips, jnp.concatenate([sums, squares], axis=1))
    means, scales = finish_stats(totals, counts, LROWS * (C2 // GROUPS))
    active = normalize(down, means, scales, gain_second, bias_second)

    flat = active.reshape(-1, C2)
    latent = jnp.dot(flat, project, preferred_element_type=jnp.float32) + project_bias
    return latent.astype(jnp.bfloat16).reshape(how_many, LROWS, LAT)


def per_device(
    pixels,
    tile_clip,
    tile_encoder,
    slot_owner,
    conv_first,
    gain_first,
    bias_first,
    conv_down,
    gain_second,
    bias_second,
    project,
    project_bias,
):
    weights = (
        conv_first,
        gain_first,
        bias_first,
        conv_down,
        gain_second,
        bias_second,
        project,
        project_bias,
    )
    group_width = lax.axis_size("dev")
    slots = slot_owner.shape[0]
    capacity = slots // group_width
    encoder = tile_encoder[:, 0]
    owner = slot_owner[:, 0]
    place = encoder * capacity + arrival_rank(encoder)
    target = owner * capacity + arrival_rank(owner)

    how_many = pixels.shape[0]
    tiles = pixels.reshape(how_many, FR, HT, WT, 3)
    latents = encode(tiles, tile_clip, weights)

    latents, target = lax.optimization_barrier((latents, target))
    outgoing = route(latents.reshape(how_many, LROWS * LAT), place, slots)
    arrived = lax.all_to_all(
        outgoing.reshape(group_width, capacity, LROWS, LAT),
        "dev",
        split_axis=0,
        concat_axis=0,
        tiled=True,
    ).reshape(slots, LROWS, LAT)
    forward = route(arrived.reshape(slots, LROWS * LAT), target, slots)
    received = lax.all_to_all(
        forward.reshape(group_width, capacity, LROWS, LAT),
        "dev",
        split_axis=0,
        concat_axis=0,
        tiled=True,
    )
    return received.reshape(slots * LROWS, LAT)


def solution(mesh):
    in_specs = (
        P(AXES, None),
        P(AXES),
        P(AXES, None),
        P(AXES, None),
        P(),
        P(),
        P(),
        P(),
        P(),
        P(),
        P(),
        P(),
    )
    out_specs = P(AXES, None)
    return jax.shard_map(
        per_device, mesh=mesh, in_specs=in_specs, out_specs=out_specs, check_vma=False
    )
```

```python
import jax
import jax.numpy as jnp
from jax import lax
from jax.sharding import PartitionSpec as P

C1 = 128
C2 = 256
LAT = 128
GROUPS = 32
FR = 2
HT = 8
WT = 8
LROWS = 32
AXES = ("slab", "dev")


epsilon = 1e-05
layout = ("NDHWC", "DHWIO", "NDHWC")
precise = lax.Precision.HIGHEST


def conv_local(inputs, kernel, stride):
    return lax.conv_general_dilated(
        inputs,
        kernel,
        (1, stride, stride),
        ((2, 0), (1, 1), (1, 1)),
        dimension_numbers=layout,
        preferred_element_type=jnp.float32,
    )


def group_sums(values):
    tiles = values.shape[0]
    width = values.shape[-1]
    grouped = values.reshape(tiles, -1, GROUPS, width // GROUPS)
    return (jnp.sum(grouped, axis=(1, 3)), jnp.sum(grouped * grouped, axis=(1, 3)))


def shifted(x, shift, n):
    if shift > 0:
        perm = [(i, i + shift) for i in range(n - shift)]
    else:
        perm = [(i, i + shift) for i in range(-shift, n)]
    return lax.ppermute(x, AXES, perm)


def clip_totals(clips, stats):
    n = lax.axis_size("slab") * lax.axis_size("dev")
    member = (clips[:, None] == clips[None, :]).astype(jnp.float32)
    own = jnp.dot(member, stats, precision=precise)
    clip_f = clips.astype(jnp.float32)
    to_right = jnp.concatenate([clip_f[-1:], own[-1]])
    to_left = jnp.concatenate([clip_f[:1], own[0]])
    mine = jnp.stack([to_left, to_right])
    from_left = shifted(mine, 2, n)
    from_right = shifted(mine, -2, n)
    bundle = jnp.concatenate([mine, from_left, from_right])
    partner = lax.ppermute(bundle, AXES, [(i, i ^ 1) for i in range(n)])
    odd = (lax.axis_index(AXES) % 2) == 1
    left_near = jnp.where(odd, partner[1], partner[3])
    left_far = from_left[1]
    right_near = jnp.where(odd, partner[4], partner[0])
    right_far = from_right[0]
    received = jnp.stack([left_near, left_far, right_near, right_far])
    match = (clip_f[:, None] == received[None, :, 0]).astype(jnp.float32)
    return own + jnp.dot(match, received[:, 1:], precision=precise)


def finish_stats(totals, counts, per_tile):
    voxels = counts * per_tile
    means = totals[:, :GROUPS] / voxels
    variance = totals[:, GROUPS : 2 * GROUPS] / voxels - means * means
    return (means, lax.rsqrt(variance + epsilon))


def normalize(values, means, scales, gain, offset):
    tiles = values.shape[0]
    width = values.shape[-1]
    grouped = values.astype(jnp.float32).reshape(tiles, -1, GROUPS, width // GROUPS)
    scaled = (grouped - means[:, None, :, None]) * scales[:, None, :, None]
    result = scaled.reshape(values.shape) * gain + offset
    return jax.nn.silu(result).astype(jnp.bfloat16)


def arrival_rank(targets):
    order = jnp.arange(targets.shape[0])
    earlier = (targets[None, :] == targets[:, None]) & (order[None, :] < order[:, None])
    return jnp.sum(earlier.astype(jnp.int32), axis=1)


def route(values, place, slots):
    pick = (jnp.arange(slots, dtype=jnp.int32)[:, None] == place[None, :]).astype(values.dtype)
    return jnp.dot(pick, values, preferred_element_type=jnp.float32).astype(values.dtype)


def encode(tiles, clips, weights):
    (
        conv_first,
        gain_first,
        bias_first,
        conv_down,
        gain_second,
        bias_second,
        project,
        project_bias,
    ) = weights
    how_many = tiles.shape[0]
    ones = jnp.ones((how_many, 1), jnp.float32)

    hidden = conv_local(tiles, conv_first, 1).astype(jnp.bfloat16)
    sums, squares = group_sums(hidden.astype(jnp.float32))
    totals = clip_totals(clips, jnp.concatenate([sums, squares, ones], axis=1))
    counts = totals[:, -1:]
    means, scales = finish_stats(totals, counts, FR * HT * WT * (C1 // GROUPS))
    active = normalize(hidden, means, scales, gain_first, bias_first)

    down = conv_local(active, conv_down, 2).astype(jnp.bfloat16)
    sums, squares = group_sums(down.astype(jnp.float32))
    totals = clip_totals(clips, jnp.concatenate([sums, squares], axis=1))
    means, scales = finish_stats(totals, counts, LROWS * (C2 // GROUPS))
    active = normalize(down, means, scales, gain_second, bias_second)

    flat = active.reshape(-1, C2)
    latent = jnp.dot(flat, project, preferred_element_type=jnp.float32) + project_bias
    return latent.astype(jnp.bfloat16).reshape(how_many, LROWS, LAT)


def per_device(
    pixels,
    tile_clip,
    tile_encoder,
    slot_owner,
    conv_first,
    gain_first,
    bias_first,
    conv_down,
    gain_second,
    bias_second,
    project,
    project_bias,
):
    weights = (
        conv_first,
        gain_first,
        bias_first,
        conv_down,
        gain_second,
        bias_second,
        project,
        project_bias,
    )
    group_width = lax.axis_size("dev")
    slots = slot_owner.shape[0]
    capacity = slots // group_width
    encoder = tile_encoder[:, 0]
    owner = slot_owner[:, 0]
    place = encoder * capacity + arrival_rank(encoder)
    target = owner * capacity + arrival_rank(owner)

    how_many = pixels.shape[0]
    tiles = pixels.reshape(how_many, FR, HT, WT, 3)
    latents = encode(tiles, tile_clip, weights)

    source = jnp.argmax(target[None, :] == jnp.arange(slots, dtype=jnp.int32)[:, None], axis=1)
    latents, source = lax.optimization_barrier((latents, source.astype(jnp.int32)))
    outgoing = route(latents.reshape(how_many, LROWS * LAT), place, slots)
    arrived = lax.all_to_all(
        outgoing.reshape(group_width, capacity, LROWS, LAT),
        "dev",
        split_axis=0,
        concat_axis=0,
        tiled=True,
    ).reshape(slots, LROWS, LAT)
    forward = jnp.take(arrived.reshape(slots, LROWS * LAT), source, axis=0)
    received = lax.all_to_all(
        forward.reshape(group_width, capacity, LROWS, LAT),
        "dev",
        split_axis=0,
        concat_axis=0,
        tiled=True,
    )
    return received.reshape(slots * LROWS, LAT)


def solution(mesh):
    in_specs = (
        P(AXES, None),
        P(AXES),
        P(AXES, None),
        P(AXES, None),
        P(),
        P(),
        P(),
        P(),
        P(),
        P(),
        P(),
        P(),
    )
    out_specs = P(AXES, None)
    return jax.shard_map(
        per_device, mesh=mesh, in_specs=in_specs, out_specs=out_specs, check_vma=False
    )
```

```python
import jax
import jax.numpy as jnp
from jax import lax
from jax.sharding import PartitionSpec as P

C1 = 128
C2 = 256
LAT = 128
GROUPS = 32
FR = 2
HT = 8
WT = 8
LROWS = 32
AXES = ("slab", "dev")


epsilon = 1e-05
layout = ("NDHWC", "DHWIO", "NDHWC")
precise = lax.Precision.HIGHEST


def conv_local(inputs, kernel, stride):
    return lax.conv_general_dilated(
        inputs,
        kernel,
        (1, stride, stride),
        ((2, 0), (1, 1), (1, 1)),
        dimension_numbers=layout,
        preferred_element_type=jnp.float32,
    )


def group_sums(values):
    tiles = values.shape[0]
    width = values.shape[-1]
    grouped = values.reshape(tiles, -1, GROUPS, width // GROUPS)
    return (jnp.sum(grouped, axis=(1, 3)), jnp.sum(grouped * grouped, axis=(1, 3)))


def shifted(x, shift, n):
    if shift > 0:
        perm = [(i, i + shift) for i in range(n - shift)]
    else:
        perm = [(i, i + shift) for i in range(-shift, n)]
    return lax.ppermute(x, AXES, perm)


def clip_totals(clips, stats):
    n = lax.axis_size("slab") * lax.axis_size("dev")
    member = (clips[:, None] == clips[None, :]).astype(jnp.float32)
    own = jnp.dot(member, stats, precision=precise)
    clip_f = clips.astype(jnp.float32)
    to_right = jnp.concatenate([clip_f[-1:], own[-1]])
    to_left = jnp.concatenate([clip_f[:1], own[0]])
    mine = jnp.stack([to_left, to_right])
    from_left = shifted(mine, 2, n)
    from_right = shifted(mine, -2, n)
    bundle = jnp.concatenate([mine, from_left, from_right])
    partner = lax.ppermute(bundle, AXES, [(i, i ^ 1) for i in range(n)])
    odd = (lax.axis_index(AXES) % 2) == 1
    left_near = jnp.where(odd, partner[1], partner[3])
    left_far = from_left[1]
    right_near = jnp.where(odd, partner[4], partner[0])
    right_far = from_right[0]
    received = jnp.stack([left_near, left_far, right_near, right_far])
    match = (clip_f[:, None] == received[None, :, 0]).astype(jnp.float32)
    return own + jnp.dot(match, received[:, 1:], precision=precise)


def finish_stats(totals, counts, per_tile):
    voxels = counts * per_tile
    means = totals[:, :GROUPS] / voxels
    variance = totals[:, GROUPS : 2 * GROUPS] / voxels - means * means
    return (means, lax.rsqrt(variance + epsilon))


def normalize(values, means, scales, gain, offset):
    tiles = values.shape[0]
    width = values.shape[-1]
    grouped = values.astype(jnp.float32).reshape(tiles, -1, GROUPS, width // GROUPS)
    scaled = (grouped - means[:, None, :, None]) * scales[:, None, :, None]
    result = scaled.reshape(values.shape) * gain + offset
    return jax.nn.silu(result).astype(jnp.bfloat16)


def arrival_rank(targets):
    order = jnp.arange(targets.shape[0])
    earlier = (targets[None, :] == targets[:, None]) & (order[None, :] < order[:, None])
    return jnp.sum(earlier.astype(jnp.int32), axis=1)


def route(values, place, slots):
    pick = (jnp.arange(slots, dtype=jnp.int32)[:, None] == place[None, :]).astype(values.dtype)
    return jnp.dot(pick, values, preferred_element_type=jnp.float32).astype(values.dtype)


def encode(tiles, clips, weights):
    (
        conv_first,
        gain_first,
        bias_first,
        conv_down,
        gain_second,
        bias_second,
        project,
        project_bias,
    ) = weights
    how_many = tiles.shape[0]
    ones = jnp.ones((how_many, 1), jnp.float32)

    hidden = conv_local(tiles, conv_first, 1).astype(jnp.bfloat16)
    sums, squares = group_sums(hidden.astype(jnp.float32))
    totals = clip_totals(clips, jnp.concatenate([sums, squares, ones], axis=1))
    counts = totals[:, -1:]
    means, scales = finish_stats(totals, counts, FR * HT * WT * (C1 // GROUPS))
    active = normalize(hidden, means, scales, gain_first, bias_first)

    down = conv_local(active, conv_down, 2).astype(jnp.bfloat16)
    sums, squares = group_sums(down.astype(jnp.float32))
    totals = clip_totals(clips, jnp.concatenate([sums, squares], axis=1))
    means, scales = finish_stats(totals, counts, LROWS * (C2 // GROUPS))
    active = normalize(down, means, scales, gain_second, bias_second)

    latent = jnp.einsum("tfhwc,cd->tfhwd", active, project, preferred_element_type=jnp.float32)
    return (latent + project_bias).astype(jnp.bfloat16).reshape(how_many, LROWS, LAT)


def per_device(
    pixels,
    tile_clip,
    tile_encoder,
    slot_owner,
    conv_first,
    gain_first,
    bias_first,
    conv_down,
    gain_second,
    bias_second,
    project,
    project_bias,
):
    weights = (
        conv_first,
        gain_first,
        bias_first,
        conv_down,
        gain_second,
        bias_second,
        project,
        project_bias,
    )
    group_width = lax.axis_size("dev")
    slots = slot_owner.shape[0]
    capacity = slots // group_width
    encoder = tile_encoder[:, 0]
    owner = slot_owner[:, 0]
    place = encoder * capacity + arrival_rank(encoder)
    target = owner * capacity + arrival_rank(owner)

    how_many = pixels.shape[0]
    tiles = pixels.reshape(how_many, FR, HT, WT, 3)
    latents = encode(tiles, tile_clip, weights)

    latents, target = lax.optimization_barrier((latents, target))
    outgoing = route(latents.reshape(how_many, LROWS * LAT), place, slots)
    arrived = lax.all_to_all(
        outgoing.reshape(group_width, capacity, LROWS, LAT),
        "dev",
        split_axis=0,
        concat_axis=0,
        tiled=True,
    ).reshape(slots, LROWS, LAT)
    forward = route(arrived.reshape(slots, LROWS * LAT), target, slots)
    received = lax.all_to_all(
        forward.reshape(group_width, capacity, LROWS, LAT),
        "dev",
        split_axis=0,
        concat_axis=0,
        tiled=True,
    )
    return received.reshape(slots * LROWS, LAT)


def solution(mesh):
    in_specs = (
        P(AXES, None),
        P(AXES),
        P(AXES, None),
        P(AXES, None),
        P(),
        P(),
        P(),
        P(),
        P(),
        P(),
        P(),
        P(),
    )
    out_specs = P(AXES, None)
    return jax.shard_map(
        per_device, mesh=mesh, in_specs=in_specs, out_specs=out_specs, check_vma=False
    )
```
